32 devices in a mesh: dom: 4 (over y, x), dev: 8 (over z, core).
Axes of the slice: x: 2, y: 2, z: 4, core: 2. Of those that a mesh axis runs over, the one named last changes fastest.
Arguments:
- feats: bfloat16 [65536, 256], P(('dom', 'dev')), may hold values from -6 to 6
- w_self: bfloat16 [256, 256], replicated, may hold values from -0.375 to 0.375
- w_neigh: bfloat16 [256, 256], replicated, may hold values from -0.375 to 0.375
- cotangent: bfloat16 [65536, 256], P(('dom', 'dev')), may hold values from -8 to 8
- hub_rows: int32 [1024], P(('dom', 'dev')), may hold values from 0 to 2047
- send_rows: int32 [32, 32, 16], P(('dom', 'dev')), may hold values from 0 to 2047
- send_count: int32 [32, 32], P(('dom', 'dev')), may hold values from 1 to 16, as said below
- tile_dst: int32 [10240], P(('dom', 'dev')), may hold values from 0 to 15
- tile_src: int32 [10240], P(('dom', 'dev')), may hold values from 0 to 21
- tile_count: int32 [32], P(('dom', 'dev')), may hold values from 80 to 320, as said below
- tile_val: bfloat16 [10240, 128, 128], P(('dom', 'dev')), may hold values from -0.125 to 0.125
Outputs:
- out: bfloat16 [65536, 256], P(('dom', 'dev'))
- grad_x: bfloat16 [65536, 256], P(('dom', 'dev'))
- grad_ws: float32 [256, 256], replicated
- grad_wn: float32 [256, 256], replicated
The draws below stay inside these ranges and needn't reach their ends.
Inputs may be any that keep to these rules, and one draw needn't show every extreme that they name: `send_count`: in every draw some peer receives 16 live slots from every device. `tile_count`: each device's count is 320, 160 or 80; some device has 320.
All inputs are finite; a program needn't handle non-finite values.
Results may differ from the reference program's by a relative error of at most 0.0057.
Values may be sent and summed in bfloat16 or wider, within the bound.
No kernel may reach another device: no remote copies, remote signals or barrier semaphores. Data moves between devices by JAX's collectives and lax.ppermute only.
A program may use at most 256 MiB of HBM per device.

```python
import jax
import jax.numpy as jnp
from jax import lax

D = 256
H = 256
ROWS_DEV = 2048
TILES = 320
SLOTS = 16
HUB_DEV = 32
EDGE = 128
NODES = 65536
RB = 16
RECV_ROWS = 512
HUBS = 256
SRC_ROWS = 2816
SB = 22
N_DOM = 4
N_DEV = 8
DEVICES = 32


def draw_cotangent(key, part):
    rows = jnp.arange(NODES, dtype=jnp.float32)
    rising = jnp.exp(jnp.log(3.0) * rows / max(NODES - 1, 1))
    values = jax.random.normal(key, (NODES, H), jnp.float32) * rising[:, None]
    return jnp.clip(values, -8.0, 8.0).astype(jnp.bfloat16)


def draw_send_count(key, part):
    key_a, key_b = jax.random.split(jax.random.fold_in(key, 11))
    counts = jax.random.randint(key_a, (DEVICES, DEVICES), 1, SLOTS + 1)
    target = jax.random.randint(key_b, (), 0, DEVICES)
    column = jnp.arange(DEVICES)[None, :] == target
    return jnp.where(column, SLOTS, counts).astype(jnp.int32)


def draw_tile_count(key, part):
    key_a, key_b = jax.random.split(jax.random.fold_in(key, 23))
    shifts = jax.random.randint(key_a, (DEVICES,), 0, 3)
    counts = TILES // jnp.left_shift(jnp.int32(1), shifts)
    target = jax.random.randint(key_b, (), 0, DEVICES)
    return jnp.where(jnp.arange(DEVICES) == target, TILES, counts).astype(jnp.int32)


def plant(entries, key, least, top_value):
    index_at = [jax.random.randint(jax.random.fold_in(key, axis), (), 0, length) for axis, length in enumerate(entries.shape)]
    widest = entries.shape.index(max(entries.shape))
    beside = index_at[:widest] + [(index_at[widest] + 1) % entries.shape[widest]] + index_at[widest + 1:]
    return entries.at[tuple(index_at)].set(least).at[tuple(beside)].set(top_value)


def block_levels(own_key, extent, shards, low, largest):
    loudness = 1.0
    for axis_at, parts in shards:
        draws = jax.random.uniform(jax.random.fold_in(jax.random.fold_in(own_key, 6), axis_at), (parts,), jnp.float32, low / len(shards), largest / len(shards))
        loudness = loudness * jnp.repeat(jnp.exp(draws), extent[axis_at] // parts).reshape((-1,) + (1,) * (len(extent) - 1 - axis_at))
    return loudness


def centred(own_key, dims, deviation, reach, cuts=(), kind=jnp.bfloat16):
    drawn = deviation * jax.random.normal(own_key, dims, jnp.float32)
    if cuts:
        drawn = drawn * block_levels(own_key, dims, cuts, -0.22, 0.18)
    return jnp.clip(drawn, -reach, reach).astype(kind)


def setup_inputs(seed: int = 0) -> dict:
    seeds = jax.random.split(jax.random.key(seed), 12)
    feats = centred(seeds[0], (NODES, D), 1.0, 6.0, ((0, 32),))
    w_self = centred(seeds[1], (D, H), D ** -0.5, 0.375)
    w_neigh = centred(seeds[2], (D, H), D ** -0.5, 0.375)
    cotangent = draw_cotangent(jax.random.fold_in(seeds[11], 71), 0)
    hub_rows = plant(jax.random.randint(seeds[4], (DEVICES * HUB_DEV,), 0, ROWS_DEV), jax.random.fold_in(seeds[4], 1), 0, ROWS_DEV - 1).astype(jnp.int32)
    send_rows = plant(jax.random.randint(seeds[5], (DEVICES, DEVICES, SLOTS), 0, ROWS_DEV), jax.random.fold_in(seeds[5], 1), 0, ROWS_DEV - 1).astype(jnp.int32)
    send_count = draw_send_count(jax.random.fold_in(seeds[11], 71), 0)
    tile_dst = plant(jax.random.randint(seeds[7], (DEVICES * TILES,), 0, RB), jax.random.fold_in(seeds[7], 1), 0, RB - 1).astype(jnp.int32)
    tile_src = plant(jax.random.randint(seeds[8], (DEVICES * TILES,), 0, SB), jax.random.fold_in(seeds[8], 1), 0, SB - 1).astype(jnp.int32)
    tile_count = draw_tile_count(jax.random.fold_in(seeds[11], 71), 0)
    tile_val = centred(seeds[10], (DEVICES * TILES, EDGE, EDGE), (EDGE * TILES // RB) ** -0.5, 0.125, ((0, 32),))
    return dict(feats=feats, w_self=w_self, w_neigh=w_neigh, cotangent=cotangent, hub_rows=hub_rows, send_rows=send_rows, send_count=send_count, tile_dst=tile_dst, tile_src=tile_src, tile_count=tile_count, tile_val=tile_val)


def reference(feats, w_self, w_neigh, cotangent, hub_rows, send_rows, send_count, tile_dst, tile_src, tile_count, tile_val):
    local_x = feats.reshape(DEVICES, ROWS_DEV, D)
    hub_index = hub_rows.reshape(DEVICES, HUB_DEV)
    hub_feats = jax.vmap(lambda x, r: x[r])(local_x, hub_index)
    hub_group = hub_feats.reshape(N_DOM, HUBS, D)
    live = jnp.arange(SLOTS, dtype=jnp.int32)[None, None, :] < send_count[:, :, None]
    sent = jax.vmap(lambda x, r: x[r])(local_x, send_rows)
    sent = jnp.where(live[:, :, :, None], sent, jnp.zeros((), jnp.bfloat16))
    received = jnp.swapaxes(sent, 0, 1).reshape(DEVICES, RECV_ROWS, D)
    dst_all = tile_dst.reshape(DEVICES, TILES)
    src_all = tile_src.reshape(DEVICES, TILES)
    val_all = tile_val.reshape(DEVICES, TILES, EDGE, EDGE)
    tile_ids = jnp.arange(TILES, dtype=jnp.int32)

    def forward_one(index):
        source = jnp.concatenate([local_x[index], received[index], hub_group[index // N_DEV]], axis=0)
        picked = source.reshape(SB, EDGE, D)[src_all[index]].astype(jnp.float32)
        terms = jnp.einsum('tij,tjd->tid', val_all[index].astype(jnp.float32), picked)
        terms = jnp.where((tile_ids < tile_count[index])[:, None, None], terms, jnp.float32(0.0))
        summed = jax.ops.segment_sum(terms, dst_all[index], num_segments=RB)
        return summed.reshape(ROWS_DEV, D).astype(jnp.bfloat16)
    agg = lax.map(forward_one, jnp.arange(DEVICES, dtype=jnp.int32)).reshape(NODES, D)
    pre = jnp.dot(feats, w_self, preferred_element_type=jnp.float32) + jnp.dot(agg, w_neigh, preferred_element_type=jnp.float32)
    sig = jax.nn.sigmoid(pre)
    out = (pre * sig).astype(jnp.bfloat16)
    dpre = (cotangent.astype(jnp.float32) * sig * (1.0 + pre * (1.0 - sig))).astype(jnp.bfloat16)
    scale = 1.0 / jnp.sqrt(jnp.float32(NODES))
    grad_ws = jnp.dot(feats.T, dpre, preferred_element_type=jnp.float32) * scale
    grad_wn = jnp.dot(agg.T, dpre, preferred_element_type=jnp.float32) * scale
    dagg = jnp.dot(dpre, w_neigh.T, preferred_element_type=jnp.float32).astype(jnp.bfloat16)
    dagg_dev = dagg.reshape(DEVICES, ROWS_DEV, D)

    def backward_one(index):
        spread = dagg_dev[index].reshape(RB, EDGE, D)[dst_all[index]].astype(jnp.float32)
        terms = jnp.einsum('tij,tid->tjd', val_all[index].astype(jnp.float32), spread)
        terms = jnp.where((tile_ids < tile_count[index])[:, None, None], terms, jnp.float32(0.0))
        return jax.ops.segment_sum(terms, src_all[index], num_segments=SB).reshape(SRC_ROWS, D)
    dsource = lax.map(backward_one, jnp.arange(DEVICES, dtype=jnp.int32))
    own = dsource[:, :ROWS_DEV]
    back = dsource[:, ROWS_DEV:ROWS_DEV + RECV_ROWS].reshape(DEVICES, DEVICES, SLOTS, D)
    hub_part = dsource[:, ROWS_DEV + RECV_ROWS:]
    returned = jnp.where(live[:, :, :, None], jnp.swapaxes(back, 0, 1), jnp.float32(0.0))
    grad = jnp.dot(dpre, w_self.T, preferred_element_type=jnp.float32).reshape(DEVICES, ROWS_DEV, D) + own
    grad = jax.vmap(lambda z, r, v: z.at[r.reshape(-1)].add(v.reshape(-1, D)))(grad, send_rows, returned)
    hub_sum = hub_part.reshape(N_DOM, N_DEV, HUBS, D).sum(axis=1).reshape(DEVICES, HUB_DEV, D)
    grad = jax.vmap(lambda z, r, v: z.at[r].add(v))(grad, hub_index, hub_sum)
    grad_x = grad.reshape(NODES, D).astype(jnp.bfloat16)
    return (out, grad_x, grad_ws, grad_wn)
```

```python
import functools

import jax
import jax.numpy as jnp
from jax import lax
from jax.experimental import pallas as pl
from jax.experimental.pallas import tpu as pltpu
from jax.sharding import PartitionSpec as P


def _tile_block(tiles):
    for size in (16, 8, 4, 2, 1):
        if tiles % size == 0:
            return size
    return 1


def _agg_kernel(src_ref, dst_ref, cnt_ref, val_ref, source_ref, out_ref, acc_ref, *, tb, edge, last_src):
    i = pl.program_id(0)

    @pl.when(i == 0)
    def _():
        acc_ref[...] = jnp.zeros_like(acc_ref)

    count = cnt_ref[0]
    last_dst = acc_ref.shape[0] // edge - 1

    def body(k, carry):
        t = i * tb + k

        @pl.when(t < count)
        def _():
            s = jnp.clip(src_ref[t], 0, last_src)
            d = jnp.clip(dst_ref[t], 0, last_dst)
            x = source_ref[pl.ds(pl.multiple_of(s * edge, edge), edge), :]
            rows = pl.ds(pl.multiple_of(d * edge, edge), edge)
            acc_ref[rows, :] += jnp.dot(val_ref[k], x, preferred_element_type=jnp.float32)

        return carry

    lax.fori_loop(0, tb, body, 0, unroll=True)

    @pl.when(i == pl.num_programs(0) - 1)
    def _():
        out_ref[...] = acc_ref[...].astype(out_ref.dtype)


def _back_kernel(src_ref, dst_ref, cnt_ref, val_ref, dagg_ref, out_ref, *, tb, edge, last_dst):
    i = pl.program_id(0)

    @pl.when(i == 0)
    def _():
        out_ref[...] = jnp.zeros_like(out_ref)

    count = cnt_ref[0]
    last_src = out_ref.shape[0] // edge - 1

    def body(k, carry):
        t = i * tb + k

        @pl.when(t < count)
        def _():
            s = jnp.clip(src_ref[t], 0, last_src)
            d = jnp.clip(dst_ref[t], 0, last_dst)
            y = dagg_ref[pl.ds(pl.multiple_of(d * edge, edge), edge), :]
            rows = pl.ds(pl.multiple_of(s * edge, edge), edge)
            term = lax.dot_general(
                val_ref[k], y, (((0,), (0,)), ((), ())), preferred_element_type=jnp.float32
            )
            out_ref[rows, :] += term

        return carry

    lax.fori_loop(0, tb, body, 0, unroll=True)


def _val_map(tb):
    def index_map(i, src, dst, cnt):
        last = jnp.maximum(cnt[0] - 1, 0) // tb
        return (jnp.minimum(i, last), 0, 0)

    return index_map


def tile_aggregate(tile_src, tile_dst, tile_count, tile_val, source, rows):
    tiles, edge, _ = tile_val.shape
    width = source.shape[1]
    tb = _tile_block(tiles)
    kernel = functools.partial(_agg_kernel, tb=tb, edge=edge, last_src=source.shape[0] // edge - 1)
    return pl.pallas_call(
        kernel,
        out_shape=jax.ShapeDtypeStruct((rows, width), jnp.bfloat16),
        grid_spec=pltpu.PrefetchScalarGridSpec(
            num_scalar_prefetch=3,
            grid=(tiles // tb,),
            in_specs=[
                pl.BlockSpec((tb, edge, edge), _val_map(tb)),
                pl.BlockSpec(source.shape, lambda i, s, d, c: (0, 0)),
            ],
            out_specs=pl.BlockSpec((rows, width), lambda i, s, d, c: (0, 0)),
            scratch_shapes=[pltpu.VMEM((rows, width), jnp.float32)],
        ),
        compiler_params=pltpu.CompilerParams(dimension_semantics=("arbitrary",)),
    )(tile_src, tile_dst, tile_count, tile_val, source)


def tile_backward(tile_src, tile_dst, tile_count, tile_val, dagg, src_rows):
    tiles, edge, _ = tile_val.shape
    width = dagg.shape[1]
    tb = _tile_block(tiles)
    kernel = functools.partial(_back_kernel, tb=tb, edge=edge, last_dst=dagg.shape[0] // edge - 1)
    return pl.pallas_call(
        kernel,
        out_shape=jax.ShapeDtypeStruct((src_rows, width), jnp.float32),
        grid_spec=pltpu.PrefetchScalarGridSpec(
            num_scalar_prefetch=3,
            grid=(tiles // tb,),
            in_specs=[
                pl.BlockSpec((tb, edge, edge), _val_map(tb)),
                pl.BlockSpec(dagg.shape, lambda i, s, d, c: (0, 0)),
            ],
            out_specs=pl.BlockSpec((src_rows, width), lambda i, s, d, c: (0, 0)),
        ),
        compiler_params=pltpu.CompilerParams(dimension_semantics=("arbitrary",)),
    )(tile_src, tile_dst, tile_count, tile_val, dagg)


def body(
    feats,
    w_self,
    w_neigh,
    cotangent,
    hub_rows,
    send_rows,
    send_count,
    tile_dst,
    tile_src,
    tile_count,
    tile_val,
):
    edge = tile_val.shape[1]
    rows, width = feats.shape
    peers = send_rows.shape[1]
    slots = send_rows.shape[2]
    group = lax.axis_size("dev")
    hubs_dev = hub_rows.shape[0]

    own_hubs = feats[hub_rows]
    hub_out = jnp.broadcast_to(own_hubs[None], (group, hubs_dev, width))
    hub_table = lax.all_to_all(hub_out, "dev", split_axis=0, concat_axis=0, tiled=True)
    hub_table = hub_table.reshape(group * hubs_dev, width)

    live = lax.broadcasted_iota(jnp.int32, (peers, slots), 1) < send_count[0][:, None]
    outgoing = jnp.where(live[:, :, None], feats[send_rows[0]], jnp.zeros((), jnp.bfloat16))
    incoming = lax.all_to_all(outgoing, ("dom", "dev"), split_axis=0, concat_axis=0, tiled=True)
    source = jnp.concatenate([feats, incoming.reshape(peers * slots, width), hub_table], axis=0)

    agg = tile_aggregate(tile_src, tile_dst, tile_count, tile_val, source, rows)

    pre = jnp.dot(feats, w_self, preferred_element_type=jnp.float32) + jnp.dot(
        agg, w_neigh, preferred_element_type=jnp.float32
    )
    sig = jax.nn.sigmoid(pre)
    out = (pre * sig).astype(jnp.bfloat16)
    dpre = (cotangent.astype(jnp.float32) * sig * (1.0 + pre * (1.0 - sig))).astype(jnp.bfloat16)

    contract_rows = (((0,), (0,)), ((), ()))
    local_ws = lax.dot_general(feats, dpre, contract_rows, preferred_element_type=jnp.float32)
    local_wn = lax.dot_general(agg, dpre, contract_rows, preferred_element_type=jnp.float32)
    partial = jnp.concatenate([local_ws, local_wn], axis=0)
    parts = partial.reshape(peers, -1, width)
    gathered = lax.all_to_all(parts, ("dom", "dev"), split_axis=0, concat_axis=0, tiled=True)
    piece = jnp.sum(gathered, axis=0)
    spread_piece = jnp.broadcast_to(piece[None], (peers,) + piece.shape)
    summed = lax.all_to_all(spread_piece, ("dom", "dev"), split_axis=0, concat_axis=0, tiled=True)
    summed = summed.reshape(partial.shape)
    scale = 1.0 / jnp.sqrt(jnp.float32(rows * peers))
    grad_ws = summed[: w_self.shape[0]] * scale
    grad_wn = summed[w_self.shape[0] :] * scale

    contract_cols = (((1,), (1,)), ((), ()))
    dagg = lax.dot_general(dpre, w_neigh, contract_cols, preferred_element_type=jnp.float32).astype(
        jnp.bfloat16
    )
    dsource = tile_backward(tile_src, tile_dst, tile_count, tile_val, dagg, source.shape[0])
    own = dsource[:rows]
    returning = dsource[rows : rows + peers * slots].reshape(peers, slots, width)
    hub_part = dsource[rows + peers * slots :]
    returned = lax.all_to_all(
        returning.astype(jnp.bfloat16), ("dom", "dev"), split_axis=0, concat_axis=0, tiled=True
    ).astype(jnp.float32)
    returned = jnp.where(live[:, :, None], returned, jnp.float32(0.0))
    hub_back = lax.all_to_all(
        hub_part.astype(jnp.bfloat16).reshape(group, hubs_dev, width),
        "dev",
        split_axis=0,
        concat_axis=0,
        tiled=True,
    )
    hub_back = jnp.sum(hub_back.astype(jnp.float32), axis=0)
    grad = lax.dot_general(dpre, w_self, contract_cols, preferred_element_type=jnp.float32) + own
    grad = grad.at[send_rows[0].reshape(-1)].add(returned.reshape(peers * slots, width))
    grad = grad.at[hub_rows].add(hub_back)
    return (out, grad.astype(jnp.bfloat16), grad_ws, grad_wn)


def solution(mesh):
    return jax.shard_map(
        body,
        mesh=mesh,
        in_specs=(
            P(("dom", "dev"), None),
            P(),
            P(),
            P(("dom", "dev"), None),
            P(("dom", "dev")),
            P(("dom", "dev"), None, None),
            P(("dom", "dev"), None),
            P(("dom", "dev")),
            P(("dom", "dev")),
            P(("dom", "dev")),
            P(("dom", "dev"), None, None),
        ),
        out_specs=(P(("dom", "dev"), None), P(("dom", "dev"), None), P(), P()),
        check_vma=False,
    )
```

```python
import functools

import jax
import jax.numpy as jnp
from jax import lax
from jax.experimental import pallas as pl
from jax.experimental.pallas import tpu as pltpu
from jax.sharding import PartitionSpec as P


def _tile_block(tiles):
    for size in (80, 64, 40, 32, 16, 8, 4, 2, 1):
        if tiles % size == 0:
            return size
    return 1


def _val_map(tb):
    def index_map(i, src, dst, cnt):
        last = jnp.maximum(cnt[0] - 1, 0) // tb
        return (jnp.minimum(i, last), 0, 0)
    return index_map

def _agg_kernel(src_ref, dst_ref, cnt_ref, val_ref, source_ref, out_ref, acc_ref, *, tb, edge, batch):
    i = pl.program_id(0)
    last_src = source_ref.shape[0] // edge - 1
    last_dst = acc_ref.shape[0] // edge - 1
    @pl.when(i == 0)
    def _():
        acc_ref[...] = jnp.zeros_like(acc_ref)
    count = cnt_ref[0]
    def one(t, k):
        s = jnp.clip(src_ref[t], 0, last_src)
        x = source_ref[pl.ds(pl.multiple_of(s * edge, edge), edge), :]
        return jnp.dot(val_ref[k], x, preferred_element_type=jnp.float32)
    def add(t, term):
        d = jnp.clip(dst_ref[t], 0, last_dst)
        rows = pl.ds(pl.multiple_of(d * edge, edge), edge)
        acc_ref[rows, :] += term
    full = (i + 1) * tb <= count
    @pl.when(full)
    def _():
        for k0 in range(0, tb, batch):
            terms = [one(i * tb + k, k) for k in range(k0, k0 + batch)]
            for k, term in zip(range(k0, k0 + batch), terms):
                add(i * tb + k, term)
    @pl.when(jnp.logical_and(jnp.logical_not(full), i * tb < count))
    def _():
        def body(k, carry):
            t = i * tb + k
            @pl.when(t < count)
            def _():
                add(t, one(t, k))
            return carry
        lax.fori_loop(0, tb, body, 0)
    @pl.when(i == pl.num_programs(0) - 1)
    def _():
        out_ref[...] = acc_ref[...].astype(out_ref.dtype)

def tile_aggregate(tile_src, tile_dst, tile_count, tile_val, source, rows, tb=16, batch=1):
    tiles, edge, _ = tile_val.shape
    width = source.shape[1]
    kernel = functools.partial(_agg_kernel, tb=tb, edge=edge, batch=batch)
    return pl.pallas_call(
        kernel,
        out_shape=jax.ShapeDtypeStruct((rows, width), jnp.bfloat16),
        grid_spec=pltpu.PrefetchScalarGridSpec(
            num_scalar_prefetch=3, grid=(tiles // tb,),
            in_specs=[pl.BlockSpec((tb, edge, edge), _val_map(tb)),
                      pl.BlockSpec(source.shape, lambda i, s, d, c: (0, 0))],
            out_specs=pl.BlockSpec((rows, width), lambda i, s, d, c: (0, 0)),
            scratch_shapes=[pltpu.VMEM((rows, width), jnp.float32)]),
        compiler_params=pltpu.CompilerParams(dimension_semantics=("arbitrary",)),
    )(tile_src, tile_dst, tile_count, tile_val, source)

def _back_kernel(src_ref, dst_ref, cnt_ref, val_ref, daggT_ref, out_ref, *, tb, edge, batch):
    i = pl.program_id(0)
    last_src = out_ref.shape[1] // edge - 1
    last_dst = daggT_ref.shape[1] // edge - 1
    @pl.when(i == 0)
    def _():
        out_ref[...] = jnp.zeros_like(out_ref)
    count = cnt_ref[0]
    def one(t, k):
        d = jnp.clip(dst_ref[t], 0, last_dst)
        y = daggT_ref[:, pl.ds(pl.multiple_of(d * edge, edge), edge)]
        return jnp.dot(y, val_ref[k], preferred_element_type=jnp.float32)
    def add(t, term):
        s = jnp.clip(src_ref[t], 0, last_src)
        cols = pl.ds(pl.multiple_of(s * edge, edge), edge)
        out_ref[:, cols] += term
    full = (i + 1) * tb <= count
    @pl.when(full)
    def _():
        for k0 in range(0, tb, batch):
            terms = [one(i * tb + k, k) for k in range(k0, k0 + batch)]
            for k, term in zip(range(k0, k0 + batch), terms):
                add(i * tb + k, term)
    @pl.when(jnp.logical_and(jnp.logical_not(full), i * tb < count))
    def _():
        def body(k, carry):
            t = i * tb + k
            @pl.when(t < count)
            def _():
                add(t, one(t, k))
            return carry
        lax.fori_loop(0, tb, body, 0)

def tile_backward_t(tile_src, tile_dst, tile_count, tile_val, daggT, src_rows, tb=16, batch=1):
    tiles, edge, _ = tile_val.shape
    width = daggT.shape[0]
    kernel = functools.partial(_back_kernel, tb=tb, edge=edge, batch=batch)
    return pl.pallas_call(
        kernel,
        out_shape=jax.ShapeDtypeStruct((width, src_rows), jnp.float32),
        grid_spec=pltpu.PrefetchScalarGridSpec(
            num_scalar_prefetch=3, grid=(tiles // tb,),
            in_specs=[pl.BlockSpec((tb, edge, edge), _val_map(tb)),
                      pl.BlockSpec(daggT.shape, lambda i, s, d, c: (0, 0))],
            out_specs=pl.BlockSpec((width, src_rows), lambda i, s, d, c: (0, 0))),
        compiler_params=pltpu.CompilerParams(dimension_semantics=("arbitrary",)),
    )(tile_src, tile_dst, tile_count, tile_val, daggT)


def body(
    feats,
    w_self,
    w_neigh,
    cotangent,
    hub_rows,
    send_rows,
    send_count,
    tile_dst,
    tile_src,
    tile_count,
    tile_val,
):
    edge = tile_val.shape[1]
    rows, width = feats.shape
    peers = send_rows.shape[1]
    slots = send_rows.shape[2]
    group = lax.axis_size("dev")
    hubs_dev = hub_rows.shape[0]

    own_hubs = feats[hub_rows]
    hub_out = jnp.broadcast_to(own_hubs[None], (group, hubs_dev, width))
    hub_table = lax.all_to_all(hub_out, "dev", split_axis=0, concat_axis=0, tiled=True)
    hub_table = hub_table.reshape(group * hubs_dev, width)

    live = lax.broadcasted_iota(jnp.int32, (peers, slots), 1) < send_count[0][:, None]
    outgoing = jnp.where(live[:, :, None], feats[send_rows[0]], jnp.zeros((), jnp.bfloat16))
    incoming = lax.all_to_all(outgoing, ("dom", "dev"), split_axis=0, concat_axis=0, tiled=True)
    source = jnp.concatenate([feats, incoming.reshape(peers * slots, width), hub_table], axis=0)

    tb = _tile_block(tile_val.shape[0])
    agg = tile_aggregate(tile_src, tile_dst, tile_count, tile_val, source, rows, tb=tb)

    pre = jnp.dot(feats, w_self, preferred_element_type=jnp.float32) + jnp.dot(
        agg, w_neigh, preferred_element_type=jnp.float32
    )
    sig = jax.nn.sigmoid(pre)
    out = (pre * sig).astype(jnp.bfloat16)
    dpre = (cotangent.astype(jnp.float32) * sig * (1.0 + pre * (1.0 - sig))).astype(jnp.bfloat16)

    contract_rows = (((0,), (0,)), ((), ()))
    local_ws = lax.dot_general(feats, dpre, contract_rows, preferred_element_type=jnp.float32)
    local_wn = lax.dot_general(agg, dpre, contract_rows, preferred_element_type=jnp.float32)
    partial = jnp.concatenate([local_ws, local_wn], axis=0)
    parts = partial.reshape(peers, -1, width)
    gathered = lax.all_to_all(parts, ("dom", "dev"), split_axis=0, concat_axis=0, tiled=True)
    piece = jnp.sum(gathered, axis=0)
    spread_piece = jnp.broadcast_to(piece[None], (peers,) + piece.shape)
    summed = lax.all_to_all(spread_piece, ("dom", "dev"), split_axis=0, concat_axis=0, tiled=True)
    summed = summed.reshape(partial.shape)
    scale = 1.0 / jnp.sqrt(jnp.float32(rows * peers))
    grad_ws = summed[: w_self.shape[0]] * scale
    grad_wn = summed[w_self.shape[0] :] * scale

    contract_cols = (((1,), (1,)), ((), ()))
    dagg_t = lax.dot_general(w_neigh, dpre, contract_cols, preferred_element_type=jnp.float32).astype(
        jnp.bfloat16
    )
    dsource_t = tile_backward_t(tile_src, tile_dst, tile_count, tile_val, dagg_t, source.shape[0], tb=tb)
    own = dsource_t[:, :rows].T
    returning = dsource_t[:, rows : rows + peers * slots].T.reshape(peers, slots, width)
    hub_part = dsource_t[:, rows + peers * slots :].T
    returned = lax.all_to_all(
        returning.astype(jnp.bfloat16), ("dom", "dev"), split_axis=0, concat_axis=0, tiled=True
    ).astype(jnp.float32)
    returned = jnp.where(live[:, :, None], returned, jnp.float32(0.0))
    hub_back = lax.all_to_all(
        hub_part.astype(jnp.bfloat16).reshape(group, hubs_dev, width),
        "dev",
        split_axis=0,
        concat_axis=0,
        tiled=True,
    )
    hub_back = jnp.sum(hub_back.astype(jnp.float32), axis=0)
    grad = lax.dot_general(dpre, w_self, contract_cols, preferred_element_type=jnp.float32) + own
    grad = grad.at[send_rows[0].reshape(-1)].add(returned.reshape(peers * slots, width))
    grad = grad.at[hub_rows].add(hub_back)
    return (out, grad.astype(jnp.bfloat16), grad_ws, grad_wn)


def solution(mesh):
    return jax.shard_map(
        body,
        mesh=mesh,
        in_specs=(
            P(("dom", "dev"), None),
            P(),
            P(),
            P(("dom", "dev"), None),
            P(("dom", "dev")),
            P(("dom", "dev"), None, None),
            P(("dom", "dev"), None),
            P(("dom", "dev")),
            P(("dom", "dev")),
            P(("dom", "dev")),
            P(("dom", "dev"), None, None),
        ),
        out_specs=(P(("dom", "dev"), None), P(("dom", "dev"), None), P(), P()),
        check_vma=False,
    )
```

```python
import functools

import jax
import jax.numpy as jnp
from jax import lax
from jax.experimental import pallas as pl
from jax.experimental.pallas import tpu as pltpu
from jax.sharding import PartitionSpec as P


def _tile_block(tiles):
    for size in (80, 64, 40, 32, 16, 8, 4, 2, 1):
        if tiles % size == 0:
            return size
    return 1


def _val_map(tb):
    def index_map(i, src, dst, cnt):
        last = jnp.maximum(cnt[0] - 1, 0) // tb
        return (jnp.minimum(i, last), 0, 0)
    return index_map

def _agg_kernel(src_ref, dst_ref, cnt_ref, val_ref, source_ref, out_ref, acc_ref, *, tb, edge, batch):
    i = pl.program_id(0)
    last_src = source_ref.shape[0] // edge - 1
    last_dst = acc_ref.shape[0] // edge - 1
    @pl.when(i == 0)
    def _():
        acc_ref[...] = jnp.zeros_like(acc_ref)
    count = cnt_ref[0]
    def one(t, k):
        s = jnp.clip(src_ref[t], 0, last_src)
        x = source_ref[pl.ds(pl.multiple_of(s * edge, edge), edge), :]
        return jnp.dot(val_ref[k], x, preferred_element_type=jnp.float32)
    def add(t, term):
        d = jnp.clip(dst_ref[t], 0, last_dst)
        rows = pl.ds(pl.multiple_of(d * edge, edge), edge)
        acc_ref[rows, :] += term
    full = (i + 1) * tb <= count
    @pl.when(full)
    def _():
        for k0 in range(0, tb, batch):
            terms = [one(i * tb + k, k) for k in range(k0, k0 + batch)]
            for k, term in zip(range(k0, k0 + batch), terms):
                add(i * tb + k, term)
    @pl.when(jnp.logical_and(jnp.logical_not(full), i * tb < count))
    def _():
        def body(k, carry):
            t = i * tb + k
            @pl.when(t < count)
            def _():
                add(t, one(t, k))
            return carry
        lax.fori_loop(0, tb, body, 0)
    @pl.when(i == pl.num_programs(0) - 1)
    def _():
        out_ref[...] = acc_ref[...].astype(out_ref.dtype)

def tile_aggregate(tile_src, tile_dst, tile_count, tile_val, source, rows, tb=16, batch=1):
    tiles, edge, _ = tile_val.shape
    width = source.shape[1]
    kernel = functools.partial(_agg_kernel, tb=tb, edge=edge, batch=batch)
    return pl.pallas_call(
        kernel,
        out_shape=jax.ShapeDtypeStruct((rows, width), jnp.bfloat16),
        grid_spec=pltpu.PrefetchScalarGridSpec(
            num_scalar_prefetch=3, grid=(tiles // tb,),
            in_specs=[pl.BlockSpec((tb, edge, edge), _val_map(tb)),
                      pl.BlockSpec(source.shape, lambda i, s, d, c: (0, 0))],
            out_specs=pl.BlockSpec((rows, width), lambda i, s, d, c: (0, 0)),
            scratch_shapes=[pltpu.VMEM((rows, width), jnp.float32)]),
        compiler_params=pltpu.CompilerParams(dimension_semantics=("arbitrary",)),
    )(tile_src, tile_dst, tile_count, tile_val, source)

def _back_kernel(src_ref, dst_ref, cnt_ref, val_ref, daggT_ref, out_ref, *, tb, edge, batch):
    i = pl.program_id(0)
    last_src = out_ref.shape[1] // edge - 1
    last_dst = daggT_ref.shape[1] // edge - 1
    @pl.when(i == 0)
    def _():
        out_ref[...] = jnp.zeros_like(out_ref)
    count = cnt_ref[0]
    def one(t, k):
        d = jnp.clip(dst_ref[t], 0, last_dst)
        y = daggT_ref[:, pl.ds(pl.multiple_of(d * edge, edge), edge)]
        return jnp.dot(y, val_ref[k], preferred_element_type=jnp.float32)
    def add(t, term):
        s = jnp.clip(src_ref[t], 0, last_src)
        cols = pl.ds(pl.multiple_of(s * edge, edge), edge)
        out_ref[:, cols] += term
    full = (i + 1) * tb <= count
    @pl.when(full)
    def _():
        for k0 in range(0, tb, batch):
            terms = [one(i * tb + k, k) for k in range(k0, k0 + batch)]
            for k, term in zip(range(k0, k0 + batch), terms):
                add(i * tb + k, term)
    @pl.when(jnp.logical_and(jnp.logical_not(full), i * tb < count))
    def _():
        def body(k, carry):
            t = i * tb + k
            @pl.when(t < count)
            def _():
                add(t, one(t, k))
            return carry
        lax.fori_loop(0, tb, body, 0)

def tile_backward_t(tile_src, tile_dst, tile_count, tile_val, daggT, src_rows, tb=16, batch=1):
    tiles, edge, _ = tile_val.shape
    width = daggT.shape[0]
    kernel = functools.partial(_back_kernel, tb=tb, edge=edge, batch=batch)
    return pl.pallas_call(
        kernel,
        out_shape=jax.ShapeDtypeStruct((width, src_rows), jnp.float32),
        grid_spec=pltpu.PrefetchScalarGridSpec(
            num_scalar_prefetch=3, grid=(tiles // tb,),
            in_specs=[pl.BlockSpec((tb, edge, edge), _val_map(tb)),
                      pl.BlockSpec(daggT.shape, lambda i, s, d, c: (0, 0))],
            out_specs=pl.BlockSpec((width, src_rows), lambda i, s, d, c: (0, 0))),
        compiler_params=pltpu.CompilerParams(dimension_semantics=("arbitrary",)),
    )(tile_src, tile_dst, tile_count, tile_val, daggT)


def body(
    feats,
    w_self,
    w_neigh,
    cotangent,
    hub_rows,
    send_rows,
    send_count,
    tile_dst,
    tile_src,
    tile_count,
    tile_val,
):
    edge = tile_val.shape[1]
    rows, width = feats.shape
    peers = send_rows.shape[1]
    slots = send_rows.shape[2]
    group = lax.axis_size("dev")
    hubs_dev = hub_rows.shape[0]

    own_hubs = feats[hub_rows]
    hub_out = jnp.broadcast_to(own_hubs[None], (peers, hubs_dev, width))

    live = lax.broadcasted_iota(jnp.int32, (peers, slots), 1) < send_count[0][:, None]
    outgoing = jnp.where(live[:, :, None], feats[send_rows[0]], jnp.zeros((), jnp.bfloat16))
    packed = jnp.concatenate([outgoing, hub_out], axis=1)
    arrived = lax.all_to_all(packed, ("dom", "dev"), split_axis=0, concat_axis=0, tiled=True)
    incoming = arrived[:, :slots]
    group_hubs = arrived[:, slots:].reshape(peers // group, group * hubs_dev, width)
    hub_table = lax.dynamic_index_in_dim(group_hubs, lax.axis_index("dom"), axis=0, keepdims=False)
    source = jnp.concatenate([feats, incoming.reshape(peers * slots, width), hub_table], axis=0)

    tb = _tile_block(tile_val.shape[0])
    agg = tile_aggregate(tile_src, tile_dst, tile_count, tile_val, source, rows, tb=tb)

    pre = jnp.dot(feats, w_self, preferred_element_type=jnp.float32) + jnp.dot(
        agg, w_neigh, preferred_element_type=jnp.float32
    )
    sig = jax.nn.sigmoid(pre)
    out = (pre * sig).astype(jnp.bfloat16)
    dpre = (cotangent.astype(jnp.float32) * sig * (1.0 + pre * (1.0 - sig))).astype(jnp.bfloat16)

    contract_rows = (((0,), (0,)), ((), ()))
    local_ws = lax.dot_general(feats, dpre, contract_rows, preferred_element_type=jnp.float32)
    local_wn = lax.dot_general(agg, dpre, contract_rows, preferred_element_type=jnp.float32)

    contract_cols = (((1,), (1,)), ((), ()))
    dagg_t = lax.dot_general(w_neigh, dpre, contract_cols, preferred_element_type=jnp.float32).astype(
        jnp.bfloat16
    )
    dsource_t = tile_backward_t(tile_src, tile_dst, tile_count, tile_val, dagg_t, source.shape[0], tb=tb)
    own = dsource_t[:, :rows].T
    returning = dsource_t[:, rows : rows + peers * slots].T.reshape(peers, slots, width)
    hub_part = dsource_t[:, rows + peers * slots :].T
    partial = jnp.concatenate([local_ws, local_wn], axis=0)
    parts = partial.reshape(peers, -1, width)
    back_packed = jnp.concatenate([returning, parts], axis=1)
    back = lax.all_to_all(back_packed, ("dom", "dev"), split_axis=0, concat_axis=0, tiled=True)
    returned = jnp.where(live[:, :, None], back[:, :slots], jnp.float32(0.0))
    piece = jnp.sum(back[:, slots:], axis=0)
    hub_back = lax.all_to_all(
        hub_part.astype(jnp.bfloat16).reshape(group, hubs_dev, width),
        "dev",
        split_axis=0,
        concat_axis=0,
        tiled=True,
    )
    hub_back = jnp.sum(hub_back.astype(jnp.float32), axis=0)
    grad = lax.dot_general(dpre, w_self, contract_cols, preferred_element_type=jnp.float32) + own
    grad = grad.at[send_rows[0].reshape(-1)].add(returned.reshape(peers * slots, width))
    grad = grad.at[hub_rows].add(hub_back)
    spread_piece = jnp.broadcast_to(piece[None], (peers,) + piece.shape)
    summed = lax.all_to_all(spread_piece, ("dom", "dev"), split_axis=0, concat_axis=0, tiled=True)
    summed = summed.reshape(partial.shape)
    scale = 1.0 / jnp.sqrt(jnp.float32(rows * peers))
    grad_ws = summed[: w_self.shape[0]] * scale
    grad_wn = summed[w_self.shape[0] :] * scale
    return (out, grad.astype(jnp.bfloat16), grad_ws, grad_wn)


def solution(mesh):
    return jax.shard_map(
        body,
        mesh=mesh,
        in_specs=(
            P(("dom", "dev"), None),
            P(),
            P(),
            P(("dom", "dev"), None),
            P(("dom", "dev")),
            P(("dom", "dev"), None, None),
            P(("dom", "dev"), None),
            P(("dom", "dev")),
            P(("dom", "dev")),
            P(("dom", "dev")),
            P(("dom", "dev"), None, None),
        ),
        out_specs=(P(("dom", "dev"), None), P(("dom", "dev"), None), P(), P()),
        check_vma=False,
    )
```

```python
import functools

import jax
import jax.numpy as jnp
from jax import lax
from jax.experimental import pallas as pl
from jax.experimental.pallas import tpu as pltpu
from jax.sharding import PartitionSpec as P


def _tile_block(tiles):
    for size in (80, 64, 40, 32, 16, 8, 4, 2, 1):
        if tiles % size == 0:
            return size
    return 1


def _val_map(tb):
    def index_map(i, src, dst, cnt):
        last = jnp.maximum(cnt[0] - 1, 0) // tb
        return (jnp.minimum(i, last), 0, 0)
    return index_map

def _agg_kernel(src_ref, dst_ref, cnt_ref, val_ref, source_ref, out_ref, acc_ref, *, tb, edge, batch):
    i = pl.program_id(0)
    last_src = source_ref.shape[0] // edge - 1
    last_dst = acc_ref.shape[0] // edge - 1
    @pl.when(i == 0)
    def _():
        acc_ref[...] = jnp.zeros_like(acc_ref)
    count = cnt_ref[0]
    def one(t, k):
        s = jnp.clip(src_ref[t], 0, last_src)
        x = source_ref[pl.ds(pl.multiple_of(s * edge, edge), edge), :]
        return jnp.dot(val_ref[k], x, preferred_element_type=jnp.float32)
    def add(t, term):
        d = jnp.clip(dst_ref[t], 0, last_dst)
        rows = pl.ds(pl.multiple_of(d * edge, edge), edge)
        acc_ref[rows, :] += term
    full = (i + 1) * tb <= count
    @pl.when(full)
    def _():
        for k0 in range(0, tb, batch):
            terms = [one(i * tb + k, k) for k in range(k0, k0 + batch)]
            for k, term in zip(range(k0, k0 + batch), terms):
                add(i * tb + k, term)
    @pl.when(jnp.logical_and(jnp.logical_not(full), i * tb < count))
    def _():
        def body(k, carry):
            t = i * tb + k
            @pl.when(t < count)
            def _():
                add(t, one(t, k))
            return carry
        lax.fori_loop(0, tb, body, 0)
    @pl.when(i == pl.num_programs(0) - 1)
    def _():
        out_ref[...] = acc_ref[...].astype(out_ref.dtype)

def tile_aggregate(tile_src, tile_dst, tile_count, tile_val, source, rows, tb=16, batch=1):
    tiles, edge, _ = tile_val.shape
    width = source.shape[1]
    kernel = functools.partial(_agg_kernel, tb=tb, edge=edge, batch=batch)
    return pl.pallas_call(
        kernel,
        out_shape=jax.ShapeDtypeStruct((rows, width), jnp.bfloat16),
        grid_spec=pltpu.PrefetchScalarGridSpec(
            num_scalar_prefetch=3, grid=(tiles // tb,),
            in_specs=[pl.BlockSpec((tb, edge, edge), _val_map(tb)),
                      pl.BlockSpec(source.shape, lambda i, s, d, c: (0, 0))],
            out_specs=pl.BlockSpec((rows, width), lambda i, s, d, c: (0, 0)),
            scratch_shapes=[pltpu.VMEM((rows, width), jnp.float32)]),
        compiler_params=pltpu.CompilerParams(dimension_semantics=("arbitrary",)),
    )(tile_src, tile_dst, tile_count, tile_val, source)

def _back_kernel(src_ref, dst_ref, cnt_ref, val_ref, daggT_ref, out_ref, *, tb, edge, batch):
    i = pl.program_id(0)
    last_src = out_ref.shape[1] // edge - 1
    last_dst = daggT_ref.shape[1] // edge - 1
    @pl.when(i == 0)
    def _():
        out_ref[...] = jnp.zeros_like(out_ref)
    count = cnt_ref[0]
    def one(t, k):
        d = jnp.clip(dst_ref[t], 0, last_dst)
        y = daggT_ref[:, pl.ds(pl.multiple_of(d * edge, edge), edge)]
        return jnp.dot(y, val_ref[k], preferred_element_type=jnp.float32)
    def add(t, term):
        s = jnp.clip(src_ref[t], 0, last_src)
        cols = pl.ds(pl.multiple_of(s * edge, edge), edge)
        out_ref[:, cols] += term
    full = (i + 1) * tb <= count
    @pl.when(full)
    def _():
        for k0 in range(0, tb, batch):
            terms = [one(i * tb + k, k) for k in range(k0, k0 + batch)]
            for k, term in zip(range(k0, k0 + batch), terms):
                add(i * tb + k, term)
    @pl.when(jnp.logical_and(jnp.logical_not(full), i * tb < count))
    def _():
        def body(k, carry):
            t = i * tb + k
            @pl.when(t < count)
            def _():
                add(t, one(t, k))
            return carry
        lax.fori_loop(0, tb, body, 0)

def tile_backward_t(tile_src, tile_dst, tile_count, tile_val, daggT, src_rows, tb=16, batch=1):
    tiles, edge, _ = tile_val.shape
    width = daggT.shape[0]
    kernel = functools.partial(_back_kernel, tb=tb, edge=edge, batch=batch)
    return pl.pallas_call(
        kernel,
        out_shape=jax.ShapeDtypeStruct((width, src_rows), jnp.float32),
        grid_spec=pltpu.PrefetchScalarGridSpec(
            num_scalar_prefetch=3, grid=(tiles // tb,),
            in_specs=[pl.BlockSpec((tb, edge, edge), _val_map(tb)),
                      pl.BlockSpec(daggT.shape, lambda i, s, d, c: (0, 0))],
            out_specs=pl.BlockSpec((width, src_rows), lambda i, s, d, c: (0, 0))),
        compiler_params=pltpu.CompilerParams(dimension_semantics=("arbitrary",)),
    )(tile_src, tile_dst, tile_count, tile_val, daggT)


def body(
    feats,
    w_self,
    w_neigh,
    cotangent,
    hub_rows,
    send_rows,
    send_count,
    tile_dst,
    tile_src,
    tile_count,
    tile_val,
):
    edge = tile_val.shape[1]
    rows, width = feats.shape
    peers = send_rows.shape[1]
    slots = send_rows.shape[2]
    group = lax.axis_size("dev")
    hubs_dev = hub_rows.shape[0]

    own_hubs = feats[hub_rows]
    hub_out = jnp.broadcast_to(own_hubs[None], (group, hubs_dev, width))
    hub_table = lax.all_to_all(hub_out, "dev", split_axis=0, concat_axis=0, tiled=True)
    hub_table = hub_table.reshape(group * hubs_dev, width)

    live = lax.broadcasted_iota(jnp.int32, (peers, slots), 1) < send_count[0][:, None]
    outgoing = jnp.where(live[:, :, None], feats[send_rows[0]], jnp.zeros((), jnp.bfloat16))
    incoming = lax.all_to_all(outgoing, ("dom", "dev"), split_axis=0, concat_axis=0, tiled=True)
    source = jnp.concatenate([feats, incoming.reshape(peers * slots, width), hub_table], axis=0)

    tb = _tile_block(tile_val.shape[0])
    agg = tile_aggregate(tile_src, tile_dst, tile_count, tile_val, source, rows, tb=tb)

    pre = jnp.dot(feats, w_self, preferred_element_type=jnp.float32) + jnp.dot(
        agg, w_neigh, preferred_element_type=jnp.float32
    )
    sig = jax.nn.sigmoid(pre)
    out = (pre * sig).astype(jnp.bfloat16)
    dpre = (cotangent.astype(jnp.float32) * sig * (1.0 + pre * (1.0 - sig))).astype(jnp.bfloat16)

    contract_rows = (((0,), (0,)), ((), ()))
    local_ws = lax.dot_general(feats, dpre, contract_rows, preferred_element_type=jnp.float32)
    local_wn = lax.dot_general(agg, dpre, contract_rows, preferred_element_type=jnp.float32)

    contract_cols = (((1,), (1,)), ((), ()))
    dagg_t = lax.dot_general(w_neigh, dpre, contract_cols, preferred_element_type=jnp.float32).astype(
        jnp.bfloat16
    )
    dsource_t = tile_backward_t(tile_src, tile_dst, tile_count, tile_val, dagg_t, source.shape[0], tb=tb)
    own = dsource_t[:, :rows].T
    returning = dsource_t[:, rows : rows + peers * slots].T.reshape(peers, slots, width)
    hub_part = dsource_t[:, rows + peers * slots :].T
    returned = lax.all_to_all(
        returning.astype(jnp.bfloat16), ("dom", "dev"), split_axis=0, concat_axis=0, tiled=True
    ).astype(jnp.float32)
    returned = jnp.where(live[:, :, None], returned, jnp.float32(0.0))
    partial = jnp.concatenate([local_ws, local_wn], axis=0)
    partial, returned = lax.optimization_barrier((partial, returned))
    parts = partial.reshape(peers, -1, width)
    gathered = lax.all_to_all(parts, ("dom", "dev"), split_axis=0, concat_axis=0, tiled=True)
    scale = 1.0 / jnp.sqrt(jnp.float32(rows * peers))
    piece = (jnp.sum(gathered, axis=0) * scale).astype(jnp.bfloat16)
    spread_piece = jnp.broadcast_to(piece[None], (peers,) + piece.shape)
    summed = lax.all_to_all(spread_piece, ("dom", "dev"), split_axis=0, concat_axis=0, tiled=True)
    summed = summed.reshape(partial.shape).astype(jnp.float32)
    grad_ws = summed[: w_self.shape[0]]
    grad_wn = summed[w_self.shape[0] :]
    hub_back = lax.all_to_all(
        hub_part.astype(jnp.bfloat16).reshape(group, hubs_dev, width),
        "dev",
        split_axis=0,
        concat_axis=0,
        tiled=True,
    )
    hub_back = jnp.sum(hub_back.astype(jnp.float32), axis=0)
    grad = lax.dot_general(dpre, w_self, contract_cols, preferred_element_type=jnp.float32) + own
    grad = grad.at[send_rows[0].reshape(-1)].add(returned.reshape(peers * slots, width))
    grad = grad.at[hub_rows].add(hub_back)
    return (out, grad.astype(jnp.bfloat16), grad_ws, grad_wn)


def solution(mesh):
    return jax.shard_map(
        body,
        mesh=mesh,
        in_specs=(
            P(("dom", "dev"), None),
            P(),
            P(),
            P(("dom", "dev"), None),
            P(("dom", "dev")),
            P(("dom", "dev"), None, None),
            P(("dom", "dev"), None),
            P(("dom", "dev")),
            P(("dom", "dev")),
            P(("dom", "dev")),
            P(("dom", "dev"), None, None),
        ),
        out_specs=(P(("dom", "dev"), None), P(("dom", "dev"), None), P(), P()),
        check_vma=False,
    )
```

```python
import functools

import jax
import jax.numpy as jnp
from jax import lax
from jax.experimental import pallas as pl
from jax.experimental.pallas import tpu as pltpu
from jax.sharding import PartitionSpec as P


def _tile_block(tiles):
    for size in (80, 64, 40, 32, 16, 8, 4, 2, 1):
        if tiles % size == 0:
            return size
    return 1


def _val_map(tb):
    def index_map(i, src, dst, cnt):
        last = jnp.maximum(cnt[0] - 1, 0) // tb
        return (jnp.minimum(i, last), 0, 0)
    return index_map

def _agg_kernel(src_ref, dst_ref, cnt_ref, val_ref, source_ref, out_ref, acc_ref, *, tb, edge, batch):
    i = pl.program_id(0)
    last_src = source_ref.shape[0] // edge - 1
    last_dst = acc_ref.shape[0] // edge - 1
    @pl.when(i == 0)
    def _():
        acc_ref[...] = jnp.zeros_like(acc_ref)
    count = cnt_ref[0]
    def one(t, k):
        s = jnp.clip(src_ref[t], 0, last_src)
        x = source_ref[pl.ds(pl.multiple_of(s * edge, edge), edge), :]
        return jnp.dot(val_ref[k], x, preferred_element_type=jnp.float32)
    def add(t, term):
        d = jnp.clip(dst_ref[t], 0, last_dst)
        rows = pl.ds(pl.multiple_of(d * edge, edge), edge)
        acc_ref[rows, :] += term
    full = (i + 1) * tb <= count
    @pl.when(full)
    def _():
        for k0 in range(0, tb, batch):
            terms = [one(i * tb + k, k) for k in range(k0, k0 + batch)]
            for k, term in zip(range(k0, k0 + batch), terms):
                add(i * tb + k, term)
    @pl.when(jnp.logical_and(jnp.logical_not(full), i * tb < count))
    def _():
        def body(k, carry):
            t = i * tb + k
            @pl.when(t < count)
            def _():
                add(t, one(t, k))
            return carry
        lax.fori_loop(0, tb, body, 0)
    @pl.when(i == pl.num_programs(0) - 1)
    def _():
        out_ref[...] = acc_ref[...].astype(out_ref.dtype)

def tile_aggregate(tile_src, tile_dst, tile_count, tile_val, source, rows, tb=16, batch=1):
    tiles, edge, _ = tile_val.shape
    width = source.shape[1]
    kernel = functools.partial(_agg_kernel, tb=tb, edge=edge, batch=batch)
    return pl.pallas_call(
        kernel,
        out_shape=jax.ShapeDtypeStruct((rows, width), jnp.bfloat16),
        grid_spec=pltpu.PrefetchScalarGridSpec(
            num_scalar_prefetch=3, grid=(tiles // tb,),
            in_specs=[pl.BlockSpec((tb, edge, edge), _val_map(tb)),
                      pl.BlockSpec(source.shape, lambda i, s, d, c: (0, 0))],
            out_specs=pl.BlockSpec((rows, width), lambda i, s, d, c: (0, 0)),
            scratch_shapes=[pltpu.VMEM((rows, width), jnp.float32)]),
        compiler_params=pltpu.CompilerParams(dimension_semantics=("arbitrary",)),
    )(tile_src, tile_dst, tile_count, tile_val, source)

def _back_kernel(src_ref, dst_ref, cnt_ref, val_ref, daggT_ref, out_ref, *, tb, edge, batch):
    i = pl.program_id(0)
    last_src = out_ref.shape[1] // edge - 1
    last_dst = daggT_ref.shape[1] // edge - 1
    @pl.when(i == 0)
    def _():
        out_ref[...] = jnp.zeros_like(out_ref)
    count = cnt_ref[0]
    def one(t, k):
        d = jnp.clip(dst_ref[t], 0, last_dst)
        y = daggT_ref[:, pl.ds(pl.multiple_of(d * edge, edge), edge)]
        return jnp.dot(y, val_ref[k], preferred_element_type=jnp.float32)
    def add(t, term):
        s = jnp.clip(src_ref[t], 0, last_src)
        cols = pl.ds(pl.multiple_of(s * edge, edge), edge)
        out_ref[:, cols] += term
    full = (i + 1) * tb <= count
    @pl.when(full)
    def _():
        for k0 in range(0, tb, batch):
            terms = [one(i * tb + k, k) for k in range(k0, k0 + batch)]
            for k, term in zip(range(k0, k0 + batch), terms):
                add(i * tb + k, term)
    @pl.when(jnp.logical_and(jnp.logical_not(full), i * tb < count))
    def _():
        def body(k, carry):
            t = i * tb + k
            @pl.when(t < count)
            def _():
                add(t, one(t, k))
            return carry
        lax.fori_loop(0, tb, body, 0)

def tile_backward_t(tile_src, tile_dst, tile_count, tile_val, daggT, src_rows, tb=16, batch=1):
    tiles, edge, _ = tile_val.shape
    width = daggT.shape[0]
    kernel = functools.partial(_back_kernel, tb=tb, edge=edge, batch=batch)
    return pl.pallas_call(
        kernel,
        out_shape=jax.ShapeDtypeStruct((width, src_rows), jnp.float32),
        grid_spec=pltpu.PrefetchScalarGridSpec(
            num_scalar_prefetch=3, grid=(tiles // tb,),
            in_specs=[pl.BlockSpec((tb, edge, edge), _val_map(tb)),
                      pl.BlockSpec(daggT.shape, lambda i, s, d, c: (0, 0))],
            out_specs=pl.BlockSpec((width, src_rows), lambda i, s, d, c: (0, 0))),
        compiler_params=pltpu.CompilerParams(dimension_semantics=("arbitrary",)),
    )(tile_src, tile_dst, tile_count, tile_val, daggT)


def one_hot_rows(index, count):
    columns = lax.broadcasted_iota(jnp.int32, (index.shape[0], count), 1)
    return (columns == index[:, None]).astype(jnp.bfloat16)


def body(
    feats,
    w_self,
    w_neigh,
    cotangent,
    hub_rows,
    send_rows,
    send_count,
    tile_dst,
    tile_src,
    tile_count,
    tile_val,
):
    edge = tile_val.shape[1]
    rows, width = feats.shape
    peers = send_rows.shape[1]
    slots = send_rows.shape[2]
    group = lax.axis_size("dev")
    hubs_dev = hub_rows.shape[0]

    hub_pick = one_hot_rows(hub_rows, rows)
    own_hubs = jnp.dot(hub_pick, feats, preferred_element_type=jnp.float32).astype(jnp.bfloat16)
    hub_out = jnp.broadcast_to(own_hubs[None], (group, hubs_dev, width))
    hub_table = lax.all_to_all(hub_out, "dev", split_axis=0, concat_axis=0, tiled=True)
    hub_table = hub_table.reshape(group * hubs_dev, width)

    live = lax.broadcasted_iota(jnp.int32, (peers, slots), 1) < send_count[0][:, None]
    send_pick = one_hot_rows(send_rows[0].reshape(-1), rows)
    send_pick = jnp.where(live.reshape(-1, 1), send_pick, jnp.zeros((), jnp.bfloat16))
    outgoing = jnp.dot(send_pick, feats, preferred_element_type=jnp.float32).astype(jnp.bfloat16)
    outgoing = outgoing.reshape(peers, slots, width)
    incoming = lax.all_to_all(outgoing, ("dom", "dev"), split_axis=0, concat_axis=0, tiled=True)
    source = jnp.concatenate([feats, incoming.reshape(peers * slots, width), hub_table], axis=0)

    tb = _tile_block(tile_val.shape[0])
    agg = tile_aggregate(tile_src, tile_dst, tile_count, tile_val, source, rows, tb=tb)

    pre = jnp.dot(feats, w_self, preferred_element_type=jnp.float32) + jnp.dot(
        agg, w_neigh, preferred_element_type=jnp.float32
    )
    sig = jax.nn.sigmoid(pre)
    out = (pre * sig).astype(jnp.bfloat16)
    dpre = (cotangent.astype(jnp.float32) * sig * (1.0 + pre * (1.0 - sig))).astype(jnp.bfloat16)

    contract_rows = (((0,), (0,)), ((), ()))
    local_ws = lax.dot_general(feats, dpre, contract_rows, preferred_element_type=jnp.float32)
    local_wn = lax.dot_general(agg, dpre, contract_rows, preferred_element_type=jnp.float32)

    contract_cols = (((1,), (1,)), ((), ()))
    dagg_t = lax.dot_general(w_neigh, dpre, contract_cols, preferred_element_type=jnp.float32).astype(
        jnp.bfloat16
    )
    dsource_t = tile_backward_t(tile_src, tile_dst, tile_count, tile_val, dagg_t, source.shape[0], tb=tb)
    own = dsource_t[:, :rows].T
    returning = dsource_t[:, rows : rows + peers * slots].T.reshape(peers, slots, width)
    hub_part = dsource_t[:, rows + peers * slots :].T
    returned = lax.all_to_all(
        returning.astype(jnp.bfloat16), ("dom", "dev"), split_axis=0, concat_axis=0, tiled=True
    )
    partial = jnp.concatenate([local_ws, local_wn], axis=0)
    partial, returned = lax.optimization_barrier((partial, returned))
    parts = partial.reshape(peers, -1, width)
    gathered = lax.all_to_all(parts, ("dom", "dev"), split_axis=0, concat_axis=0, tiled=True)
    scale = 1.0 / jnp.sqrt(jnp.float32(rows * peers))
    piece = (jnp.sum(gathered, axis=0) * scale).astype(jnp.bfloat16)
    spread_piece = jnp.broadcast_to(piece[None], (peers,) + piece.shape)
    summed = lax.all_to_all(spread_piece, ("dom", "dev"), split_axis=0, concat_axis=0, tiled=True)
    summed = summed.reshape(partial.shape).astype(jnp.float32)
    grad_ws = summed[: w_self.shape[0]]
    grad_wn = summed[w_self.shape[0] :]
    hub_back = lax.all_to_all(
        hub_part.astype(jnp.bfloat16).reshape(group, hubs_dev, width),
        "dev",
        split_axis=0,
        concat_axis=0,
        tiled=True,
    )
    hub_spread = jnp.broadcast_to(hub_pick[None], (group,) + hub_pick.shape)
    grad = lax.dot_general(dpre, w_self, contract_cols, preferred_element_type=jnp.float32) + own
    grad = grad + lax.dot_general(
        send_pick, returned.reshape(peers * slots, width), contract_rows, preferred_element_type=jnp.float32
    )
    grad = grad + lax.dot_general(
        hub_spread.reshape(group * hubs_dev, rows),
        hub_back.reshape(group * hubs_dev, width),
        contract_rows,
        preferred_element_type=jnp.float32,
    )
    return (out, grad.astype(jnp.bfloat16), grad_ws, grad_wn)


def solution(mesh):
    return jax.shard_map(
        body,
        mesh=mesh,
        in_specs=(
            P(("dom", "dev"), None),
            P(),
            P(),
            P(("dom", "dev"), None),
            P(("dom", "dev")),
            P(("dom", "dev"), None, None),
            P(("dom", "dev"), None),
            P(("dom", "dev")),
            P(("dom", "dev")),
            P(("dom", "dev")),
            P(("dom", "dev"), None, None),
        ),
        out_specs=(P(("dom", "dev"), None), P(("dom", "dev"), None), P(), P()),
        check_vma=False,
    )
```

```python
import functools

import jax
import jax.numpy as jnp
from jax import lax
from jax.experimental import pallas as pl
from jax.experimental.pallas import tpu as pltpu
from jax.sharding import PartitionSpec as P


def _tile_block(tiles):
    for size in (80, 64, 40, 32, 16, 8, 4, 2, 1):
        if tiles % size == 0:
            return size
    return 1


def _val_map(tb):
    def index_map(i, src, dst, cnt):
        last = jnp.maximum(cnt[0] - 1, 0) // tb
        return (jnp.minimum(i, last), 0, 0)
    return index_map

def _agg_kernel(src_ref, dst_ref, cnt_ref, val_ref, source_ref, out_ref, acc_ref, *, tb, edge, batch):
    i = pl.program_id(0)
    last_src = source_ref.shape[0] // edge - 1
    last_dst = acc_ref.shape[0] // edge - 1
    @pl.when(i == 0)
    def _():
        acc_ref[...] = jnp.zeros_like(acc_ref)
    count = cnt_ref[0]
    def one(t, k):
        s = jnp.clip(src_ref[t], 0, last_src)
        x = source_ref[pl.ds(pl.multiple_of(s * edge, edge), edge), :]
        return jnp.dot(val_ref[k], x, preferred_element_type=jnp.float32)
    def add(t, term):
        d = jnp.clip(dst_ref[t], 0, last_dst)
        rows = pl.ds(pl.multiple_of(d * edge, edge), edge)
        acc_ref[rows, :] += term
    full = (i + 1) * tb <= count
    @pl.when(full)
    def _():
        for k0 in range(0, tb, batch):
            terms = [one(i * tb + k, k) for k in range(k0, k0 + batch)]
            for k, term in zip(range(k0, k0 + batch), terms):
                add(i * tb + k, term)
    @pl.when(jnp.logical_and(jnp.logical_not(full), i * tb < count))
    def _():
        def body(k, carry):
            t = i * tb + k
            @pl.when(t < count)
            def _():
                add(t, one(t, k))
            return carry
        lax.fori_loop(0, tb, body, 0)
    @pl.when(i == pl.num_programs(0) - 1)
    def _():
        out_ref[...] = acc_ref[...].astype(out_ref.dtype)

def tile_aggregate(tile_src, tile_dst, tile_count, tile_val, source, rows, tb=16, batch=1):
    tiles, edge, _ = tile_val.shape
    width = source.shape[1]
    kernel = functools.partial(_agg_kernel, tb=tb, edge=edge, batch=batch)
    return pl.pallas_call(
        kernel,
        out_shape=jax.ShapeDtypeStruct((rows, width), jnp.bfloat16),
        grid_spec=pltpu.PrefetchScalarGridSpec(
            num_scalar_prefetch=3, grid=(tiles // tb,),
            in_specs=[pl.BlockSpec((tb, edge, edge), _val_map(tb)),
                      pl.BlockSpec(source.shape, lambda i, s, d, c: (0, 0))],
            out_specs=pl.BlockSpec((rows, width), lambda i, s, d, c: (0, 0)),
            scratch_shapes=[pltpu.VMEM((rows, width), jnp.float32)]),
        compiler_params=pltpu.CompilerParams(dimension_semantics=("arbitrary",)),
    )(tile_src, tile_dst, tile_count, tile_val, source)

def _back_kernel(src_ref, dst_ref, cnt_ref, val_ref, daggT_ref, own_ref, rest_ref, acc_ref, *, tb, edge, batch):
    i = pl.program_id(0)
    last_src = acc_ref.shape[1] // edge - 1
    last_dst = daggT_ref.shape[1] // edge - 1
    rows = own_ref.shape[0]

    @pl.when(i == 0)
    def _():
        acc_ref[...] = jnp.zeros_like(acc_ref)

    count = cnt_ref[0]

    def one(t, k):
        d = jnp.clip(dst_ref[t], 0, last_dst)
        y = daggT_ref[:, pl.ds(pl.multiple_of(d * edge, edge), edge)]
        return jnp.dot(y, val_ref[k], preferred_element_type=jnp.float32)

    def add(t, term):
        s = jnp.clip(src_ref[t], 0, last_src)
        cols = pl.ds(pl.multiple_of(s * edge, edge), edge)
        acc_ref[:, cols] += term

    full = (i + 1) * tb <= count

    @pl.when(full)
    def _():
        for k0 in range(0, tb, batch):
            terms = [one(i * tb + k, k) for k in range(k0, k0 + batch)]
            for k, term in zip(range(k0, k0 + batch), terms):
                add(i * tb + k, term)

    @pl.when(jnp.logical_and(jnp.logical_not(full), i * tb < count))
    def _():
        def body(k, carry):
            t = i * tb + k

            @pl.when(t < count)
            def _():
                add(t, one(t, k))

            return carry

        lax.fori_loop(0, tb, body, 0)

    @pl.when(i == pl.num_programs(0) - 1)
    def _():
        own_ref[...] = acc_ref[:, :rows].T
        rest_ref[...] = acc_ref[:, rows:].T.astype(rest_ref.dtype)


def tile_backward_t(tile_src, tile_dst, tile_count, tile_val, daggT, src_rows, tb=16, batch=1):
    tiles, edge, _ = tile_val.shape
    width, rows = daggT.shape
    kernel = functools.partial(_back_kernel, tb=tb, edge=edge, batch=batch)
    return pl.pallas_call(
        kernel,
        out_shape=(
            jax.ShapeDtypeStruct((rows, width), jnp.float32),
            jax.ShapeDtypeStruct((src_rows - rows, width), jnp.bfloat16),
        ),
        grid_spec=pltpu.PrefetchScalarGridSpec(
            num_scalar_prefetch=3, grid=(tiles // tb,),
            in_specs=[pl.BlockSpec((tb, edge, edge), _val_map(tb)),
                      pl.BlockSpec(daggT.shape, lambda i, s, d, c: (0, 0))],
            out_specs=[pl.BlockSpec((rows, width), lambda i, s, d, c: (0, 0)),
                       pl.BlockSpec((src_rows - rows, width), lambda i, s, d, c: (0, 0))],
            scratch_shapes=[pltpu.VMEM((width, src_rows), jnp.float32)]),
        compiler_params=pltpu.CompilerParams(dimension_semantics=("arbitrary",)),
    )(tile_src, tile_dst, tile_count, tile_val, daggT)


def one_hot_rows(index, count):
    columns = lax.broadcasted_iota(jnp.int32, (index.shape[0], count), 1)
    return (columns == index[:, None]).astype(jnp.bfloat16)


def body(
    feats,
    w_self,
    w_neigh,
    cotangent,
    hub_rows,
    send_rows,
    send_count,
    tile_dst,
    tile_src,
    tile_count,
    tile_val,
):
    edge = tile_val.shape[1]
    rows, width = feats.shape
    peers = send_rows.shape[1]
    slots = send_rows.shape[2]
    group = lax.axis_size("dev")
    hubs_dev = hub_rows.shape[0]

    hub_pick = one_hot_rows(hub_rows, rows)
    own_hubs = jnp.dot(hub_pick, feats, preferred_element_type=jnp.float32).astype(jnp.bfloat16)
    hub_out = jnp.broadcast_to(own_hubs[None], (group, hubs_dev, width))
    hub_table = lax.all_to_all(hub_out, "dev", split_axis=0, concat_axis=0, tiled=True)
    hub_table = hub_table.reshape(group * hubs_dev, width)

    live = lax.broadcasted_iota(jnp.int32, (peers, slots), 1) < send_count[0][:, None]
    send_pick = one_hot_rows(send_rows[0].reshape(-1), rows)
    send_pick = jnp.where(live.reshape(-1, 1), send_pick, jnp.zeros((), jnp.bfloat16))
    outgoing = jnp.dot(send_pick, feats, preferred_element_type=jnp.float32).astype(jnp.bfloat16)
    outgoing = outgoing.reshape(peers, slots, width)
    incoming = lax.all_to_all(outgoing, ("dom", "dev"), split_axis=0, concat_axis=0, tiled=True)
    source = jnp.concatenate([feats, incoming.reshape(peers * slots, width), hub_table], axis=0)

    tb = _tile_block(tile_val.shape[0])
    agg = tile_aggregate(tile_src, tile_dst, tile_count, tile_val, source, rows, tb=tb)

    pre = jnp.dot(feats, w_self, preferred_element_type=jnp.float32) + jnp.dot(
        agg, w_neigh, preferred_element_type=jnp.float32
    )
    sig = jax.nn.sigmoid(pre)
    out = (pre * sig).astype(jnp.bfloat16)
    dpre = (cotangent.astype(jnp.float32) * sig * (1.0 + pre * (1.0 - sig))).astype(jnp.bfloat16)

    contract_rows = (((0,), (0,)), ((), ()))
    local_ws = lax.dot_general(feats, dpre, contract_rows, preferred_element_type=jnp.float32)
    local_wn = lax.dot_general(agg, dpre, contract_rows, preferred_element_type=jnp.float32)

    contract_cols = (((1,), (1,)), ((), ()))
    dagg_t = lax.dot_general(w_neigh, dpre, contract_cols, preferred_element_type=jnp.float32).astype(
        jnp.bfloat16
    )
    own, rest = tile_backward_t(tile_src, tile_dst, tile_count, tile_val, dagg_t, source.shape[0], tb=tb)
    returning = rest[: peers * slots].reshape(peers, slots, width)
    hub_part = rest[peers * slots :]
    returned = lax.all_to_all(
        returning, ("dom", "dev"), split_axis=0, concat_axis=0, tiled=True
    )
    partial = jnp.concatenate([local_ws, local_wn], axis=0)
    partial, returned = lax.optimization_barrier((partial, returned))
    parts = partial.reshape(peers, -1, width)
    gathered = lax.all_to_all(parts, ("dom", "dev"), split_axis=0, concat_axis=0, tiled=True)
    scale = 1.0 / jnp.sqrt(jnp.float32(rows * peers))
    piece = (jnp.sum(gathered, axis=0) * scale).astype(jnp.bfloat16)
    spread_piece = jnp.broadcast_to(piece[None], (peers,) + piece.shape)
    summed = lax.all_to_all(spread_piece, ("dom", "dev"), split_axis=0, concat_axis=0, tiled=True)
    summed = summed.reshape(partial.shape).astype(jnp.float32)
    grad_ws = summed[: w_self.shape[0]]
    grad_wn = summed[w_self.shape[0] :]
    hub_back = lax.all_to_all(
        hub_part.reshape(group, hubs_dev, width),
        "dev",
        split_axis=0,
        concat_axis=0,
        tiled=True,
    )
    hub_spread = jnp.broadcast_to(hub_pick[None], (group,) + hub_pick.shape)
    grad = lax.dot_general(dpre, w_self, contract_cols, preferred_element_type=jnp.float32) + own
    grad = grad + lax.dot_general(
        send_pick, returned.reshape(peers * slots, width), contract_rows, preferred_element_type=jnp.float32
    )
    grad = grad + lax.dot_general(
        hub_spread.reshape(group * hubs_dev, rows),
        hub_back.reshape(group * hubs_dev, width),
        contract_rows,
        preferred_element_type=jnp.float32,
    )
    return (out, grad.astype(jnp.bfloat16), grad_ws, grad_wn)


def solution(mesh):
    return jax.shard_map(
        body,
        mesh=mesh,
        in_specs=(
            P(("dom", "dev"), None),
            P(),
            P(),
            P(("dom", "dev"), None),
            P(("dom", "dev")),
            P(("dom", "dev"), None, None),
            P(("dom", "dev"), None),
            P(("dom", "dev")),
            P(("dom", "dev")),
            P(("dom", "dev")),
            P(("dom", "dev"), None, None),
        ),
        out_specs=(P(("dom", "dev"), None), P(("dom", "dev"), None), P(), P()),
        check_vma=False,
    )
```

```python
import functools

import jax
import jax.numpy as jnp
from jax import lax
from jax.experimental import pallas as pl
from jax.experimental.pallas import tpu as pltpu
from jax.sharding import PartitionSpec as P


def _tile_block(tiles):
    for size in (80, 64, 40, 32, 16, 8, 4, 2, 1):
        if tiles % size == 0:
            return size
    return 1


def _val_map(tb):
    def index_map(i, src, dst, cnt):
        last = jnp.maximum(cnt[0] - 1, 0) // tb
        return (jnp.minimum(i, last), 0, 0)
    return index_map

def _agg_kernel(src_ref, dst_ref, cnt_ref, val_ref, source_ref, out_ref, acc_ref, *, tb, edge, batch):
    i = pl.program_id(0)
    last_src = source_ref.shape[0] // edge - 1
    last_dst = acc_ref.shape[0] // edge - 1
    @pl.when(i == 0)
    def _():
        acc_ref[...] = jnp.zeros_like(acc_ref)
    count = cnt_ref[0]
    def one(t, k):
        s = jnp.clip(src_ref[t], 0, last_src)
        x = source_ref[pl.ds(pl.multiple_of(s * edge, edge), edge), :]
        return jnp.dot(val_ref[k], x, preferred_element_type=jnp.float32)
    def add(t, term):
        d = jnp.clip(dst_ref[t], 0, last_dst)
        rows = pl.ds(pl.multiple_of(d * edge, edge), edge)
        acc_ref[rows, :] += term
    full = (i + 1) * tb <= count
    @pl.when(full)
    def _():
        for k0 in range(0, tb, batch):
            terms = [one(i * tb + k, k) for k in range(k0, k0 + batch)]
            for k, term in zip(range(k0, k0 + batch), terms):
                add(i * tb + k, term)
    @pl.when(jnp.logical_and(jnp.logical_not(full), i * tb < count))
    def _():
        def body(k, carry):
            t = i * tb + k
            @pl.when(t < count)
            def _():
                add(t, one(t, k))
            return carry
        lax.fori_loop(0, tb, body, 0)
    @pl.when(i == pl.num_programs(0) - 1)
    def _():
        out_ref[...] = acc_ref[...].astype(out_ref.dtype)

def tile_aggregate(tile_src, tile_dst, tile_count, tile_val, source, rows, tb=16, batch=1):
    tiles, edge, _ = tile_val.shape
    width = source.shape[1]
    kernel = functools.partial(_agg_kernel, tb=tb, edge=edge, batch=batch)
    return pl.pallas_call(
        kernel,
        out_shape=jax.ShapeDtypeStruct((rows, width), jnp.bfloat16),
        grid_spec=pltpu.PrefetchScalarGridSpec(
            num_scalar_prefetch=3, grid=(tiles // tb,),
            in_specs=[pl.BlockSpec((tb, edge, edge), _val_map(tb)),
                      pl.BlockSpec(source.shape, lambda i, s, d, c: (0, 0))],
            out_specs=pl.BlockSpec((rows, width), lambda i, s, d, c: (0, 0)),
            scratch_shapes=[pltpu.VMEM((rows, width), jnp.float32)]),
        compiler_params=pltpu.CompilerParams(dimension_semantics=("arbitrary",)),
    )(tile_src, tile_dst, tile_count, tile_val, source)

def _back_kernel(src_ref, dst_ref, cnt_ref, val_ref, daggT_ref, own_ref, ret_ref, hub_ref, acc_ref, *, tb, edge, batch):
    i = pl.program_id(0)
    last_src = acc_ref.shape[1] // edge - 1
    last_dst = daggT_ref.shape[1] // edge - 1
    rows = own_ref.shape[0]

    @pl.when(i == 0)
    def _():
        acc_ref[...] = jnp.zeros_like(acc_ref)

    count = cnt_ref[0]

    def one(t, k):
        d = jnp.clip(dst_ref[t], 0, last_dst)
        y = daggT_ref[:, pl.ds(pl.multiple_of(d * edge, edge), edge)]
        return jnp.dot(y, val_ref[k], preferred_element_type=jnp.float32)

    def add(t, term):
        s = jnp.clip(src_ref[t], 0, last_src)
        cols = pl.ds(pl.multiple_of(s * edge, edge), edge)
        acc_ref[:, cols] += term

    full = (i + 1) * tb <= count

    @pl.when(full)
    def _():
        for k0 in range(0, tb, batch):
            terms = [one(i * tb + k, k) for k in range(k0, k0 + batch)]
            for k, term in zip(range(k0, k0 + batch), terms):
                add(i * tb + k, term)

    @pl.when(jnp.logical_and(jnp.logical_not(full), i * tb < count))
    def _():
        def body(k, carry):
            t = i * tb + k

            @pl.when(t < count)
            def _():
                add(t, one(t, k))

            return carry

        lax.fori_loop(0, tb, body, 0)

    @pl.when(i == pl.num_programs(0) - 1)
    def _():
        own_ref[...] = acc_ref[:, :rows].T
        split = rows + ret_ref.shape[0]
        ret_ref[...] = acc_ref[:, rows:split].T.astype(ret_ref.dtype)
        hub_ref[...] = acc_ref[:, split:].T.astype(hub_ref.dtype)


def tile_backward_t(tile_src, tile_dst, tile_count, tile_val, daggT, src_rows, ret_rows, tb=16, batch=1):
    tiles, edge, _ = tile_val.shape
    width, rows = daggT.shape
    kernel = functools.partial(_back_kernel, tb=tb, edge=edge, batch=batch)
    return pl.pallas_call(
        kernel,
        out_shape=(
            jax.ShapeDtypeStruct((rows, width), jnp.float32),
            jax.ShapeDtypeStruct((ret_rows, width), jnp.bfloat16),
            jax.ShapeDtypeStruct((src_rows - rows - ret_rows, width), jnp.bfloat16),
        ),
        grid_spec=pltpu.PrefetchScalarGridSpec(
            num_scalar_prefetch=3, grid=(tiles // tb,),
            in_specs=[pl.BlockSpec((tb, edge, edge), _val_map(tb)),
                      pl.BlockSpec(daggT.shape, lambda i, s, d, c: (0, 0))],
            out_specs=[pl.BlockSpec((rows, width), lambda i, s, d, c: (0, 0)),
                       pl.BlockSpec((ret_rows, width), lambda i, s, d, c: (0, 0)),
                       pl.BlockSpec((src_rows - rows - ret_rows, width), lambda i, s, d, c: (0, 0))],
            scratch_shapes=[pltpu.VMEM((width, src_rows), jnp.float32)]),
        compiler_params=pltpu.CompilerParams(dimension_semantics=("arbitrary",)),
    )(tile_src, tile_dst, tile_count, tile_val, daggT)


def one_hot_rows(index, count):
    columns = lax.broadcasted_iota(jnp.int32, (index.shape[0], count), 1)
    return (columns == index[:, None]).astype(jnp.bfloat16)


def body(
    feats,
    w_self,
    w_neigh,
    cotangent,
    hub_rows,
    send_rows,
    send_count,
    tile_dst,
    tile_src,
    tile_count,
    tile_val,
):
    edge = tile_val.shape[1]
    rows, width = feats.shape
    peers = send_rows.shape[1]
    slots = send_rows.shape[2]
    group = lax.axis_size("dev")
    hubs_dev = hub_rows.shape[0]

    hub_pick = one_hot_rows(hub_rows, rows)
    own_hubs = jnp.dot(hub_pick, feats, preferred_element_type=jnp.float32).astype(jnp.bfloat16)
    hub_out = jnp.broadcast_to(own_hubs[None], (group, hubs_dev, width))
    hub_table = lax.all_to_all(hub_out, "dev", split_axis=0, concat_axis=0, tiled=True)
    hub_table = hub_table.reshape(group * hubs_dev, width)

    live = lax.broadcasted_iota(jnp.int32, (peers, slots), 1) < send_count[0][:, None]
    send_pick = one_hot_rows(send_rows[0].reshape(-1), rows)
    send_pick = jnp.where(live.reshape(-1, 1), send_pick, jnp.zeros((), jnp.bfloat16))
    outgoing = jnp.dot(send_pick, feats, preferred_element_type=jnp.float32).astype(jnp.bfloat16)
    outgoing = outgoing.reshape(peers, slots, width)
    incoming = lax.all_to_all(outgoing, ("dom", "dev"), split_axis=0, concat_axis=0, tiled=True)
    source = jnp.concatenate([feats, incoming.reshape(peers * slots, width), hub_table], axis=0)

    tb = _tile_block(tile_val.shape[0])
    agg = tile_aggregate(tile_src, tile_dst, tile_count, tile_val, source, rows, tb=tb)

    pre = jnp.dot(feats, w_self, preferred_element_type=jnp.float32) + jnp.dot(
        agg, w_neigh, preferred_element_type=jnp.float32
    )
    sig = jax.nn.sigmoid(pre)
    out = (pre * sig).astype(jnp.bfloat16)
    dpre = (cotangent.astype(jnp.float32) * sig * (1.0 + pre * (1.0 - sig))).astype(jnp.bfloat16)

    contract_rows = (((0,), (0,)), ((), ()))
    local_ws = lax.dot_general(feats, dpre, contract_rows, preferred_element_type=jnp.float32)
    local_wn = lax.dot_general(agg, dpre, contract_rows, preferred_element_type=jnp.float32)

    contract_cols = (((1,), (1,)), ((), ()))
    dagg_t = lax.dot_general(w_neigh, dpre, contract_cols, preferred_element_type=jnp.float32).astype(
        jnp.bfloat16
    )
    own, returning, hub_part = tile_backward_t(
        tile_src, tile_dst, tile_count, tile_val, dagg_t, source.shape[0], peers * slots, tb=tb
    )
    returning = returning.reshape(peers, slots, width)
    returned = lax.all_to_all(
        returning, ("dom", "dev"), split_axis=0, concat_axis=0, tiled=True
    )
    partial = jnp.concatenate([local_ws, local_wn], axis=0)
    partial, returned = lax.optimization_barrier((partial, returned))
    parts = partial.reshape(peers, -1, width)
    gathered = lax.all_to_all(parts, ("dom", "dev"), split_axis=0, concat_axis=0, tiled=True)
    scale = 1.0 / jnp.sqrt(jnp.float32(rows * peers))
    piece = (jnp.sum(gathered, axis=0) * scale).astype(jnp.bfloat16)
    spread_piece = jnp.broadcast_to(piece[None], (peers,) + piece.shape)
    summed = lax.all_to_all(spread_piece, ("dom", "dev"), split_axis=0, concat_axis=0, tiled=True)
    summed = summed.reshape(partial.shape).astype(jnp.float32)
    grad_ws = summed[: w_self.shape[0]]
    grad_wn = summed[w_self.shape[0] :]
    hub_back = lax.all_to_all(
        hub_part.reshape(group, hubs_dev, width),
        "dev",
        split_axis=0,
        concat_axis=0,
        tiled=True,
    )
    hub_spread = jnp.broadcast_to(hub_pick[None], (group,) + hub_pick.shape)
    grad = lax.dot_general(dpre, w_self, contract_cols, preferred_element_type=jnp.float32) + own
    grad = grad + lax.dot_general(
        send_pick, returned.reshape(peers * slots, width), contract_rows, preferred_element_type=jnp.float32
    )
    grad = grad + lax.dot_general(
        hub_spread.reshape(group * hubs_dev, rows),
        hub_back.reshape(group * hubs_dev, width),
        contract_rows,
        preferred_element_type=jnp.float32,
    )
    return (out, grad.astype(jnp.bfloat16), grad_ws, grad_wn)


def solution(mesh):
    return jax.shard_map(
        body,
        mesh=mesh,
        in_specs=(
            P(("dom", "dev"), None),
            P(),
            P(),
            P(("dom", "dev"), None),
            P(("dom", "dev")),
            P(("dom", "dev"), None, None),
            P(("dom", "dev"), None),
            P(("dom", "dev")),
            P(("dom", "dev")),
            P(("dom", "dev")),
            P(("dom", "dev"), None, None),
        ),
        out_specs=(P(("dom", "dev"), None), P(("dom", "dev"), None), P(), P()),
        check_vma=False,
    )
```

```python
import functools

import jax
import jax.numpy as jnp
from jax import lax
from jax.experimental import pallas as pl
from jax.experimental.pallas import tpu as pltpu
from jax.sharding import PartitionSpec as P


def _tile_block(tiles):
    for size in (80, 64, 40, 32, 16, 8, 4, 2, 1):
        if tiles % size == 0:
            return size
    return 1


def _val_map(tb):
    def index_map(i, src, dst, cnt):
        last = jnp.maximum(cnt[0] - 1, 0) // tb
        return (jnp.minimum(i, last), 0, 0)
    return index_map

def _agg_kernel(src_ref, dst_ref, cnt_ref, val_ref, source_ref, out_ref, acc_ref, *, tb, edge, batch):
    i = pl.program_id(0)
    last_src = source_ref.shape[0] // edge - 1
    last_dst = acc_ref.shape[0] // edge - 1
    @pl.when(i == 0)
    def _():
        acc_ref[...] = jnp.zeros_like(acc_ref)
    count = cnt_ref[0]
    def one(t, k):
        s = jnp.clip(src_ref[t], 0, last_src)
        x = source_ref[pl.ds(pl.multiple_of(s * edge, edge), edge), :]
        return jnp.dot(val_ref[k], x, preferred_element_type=jnp.float32)
    def add(t, term):
        d = jnp.clip(dst_ref[t], 0, last_dst)
        rows = pl.ds(pl.multiple_of(d * edge, edge), edge)
        acc_ref[rows, :] += term
    full = (i + 1) * tb <= count
    @pl.when(full)
    def _():
        for k0 in range(0, tb, batch):
            terms = [one(i * tb + k, k) for k in range(k0, k0 + batch)]
            for k, term in zip(range(k0, k0 + batch), terms):
                add(i * tb + k, term)
    @pl.when(jnp.logical_and(jnp.logical_not(full), i * tb < count))
    def _():
        def body(k, carry):
            t = i * tb + k
            @pl.when(t < count)
            def _():
                add(t, one(t, k))
            return carry
        lax.fori_loop(0, tb, body, 0)
    @pl.when(i == pl.num_programs(0) - 1)
    def _():
        out_ref[...] = acc_ref[...].astype(out_ref.dtype)

def tile_aggregate(tile_src, tile_dst, tile_count, tile_val, source, rows, tb=16, batch=1):
    tiles, edge, _ = tile_val.shape
    width = source.shape[1]
    kernel = functools.partial(_agg_kernel, tb=tb, edge=edge, batch=batch)
    return pl.pallas_call(
        kernel,
        out_shape=jax.ShapeDtypeStruct((rows, width), jnp.bfloat16),
        grid_spec=pltpu.PrefetchScalarGridSpec(
            num_scalar_prefetch=3, grid=(tiles // tb,),
            in_specs=[pl.BlockSpec((tb, edge, edge), _val_map(tb)),
                      pl.BlockSpec(source.shape, lambda i, s, d, c: (0, 0))],
            out_specs=pl.BlockSpec((rows, width), lambda i, s, d, c: (0, 0)),
            scratch_shapes=[pltpu.VMEM((rows, width), jnp.float32)]),
        compiler_params=pltpu.CompilerParams(dimension_semantics=("arbitrary",)),
    )(tile_src, tile_dst, tile_count, tile_val, source)

def _back_kernel(src_ref, dst_ref, cnt_ref, val_ref, daggT_ref, own_ref, ret_ref, hub_ref, acc_ref, *, tb, edge, batch):
    i = pl.program_id(0)
    last_src = acc_ref.shape[1] // edge - 1
    last_dst = daggT_ref.shape[1] // edge - 1
    rows = own_ref.shape[0]

    @pl.when(i == 0)
    def _():
        acc_ref[...] = jnp.zeros_like(acc_ref)

    count = cnt_ref[0]

    def one(t, k):
        d = jnp.clip(dst_ref[t], 0, last_dst)
        y = daggT_ref[:, pl.ds(pl.multiple_of(d * edge, edge), edge)]
        return jnp.dot(y, val_ref[k], preferred_element_type=jnp.float32)

    def add(t, term):
        s = jnp.clip(src_ref[t], 0, last_src)
        cols = pl.ds(pl.multiple_of(s * edge, edge), edge)
        acc_ref[:, cols] += term

    full = (i + 1) * tb <= count

    @pl.when(full)
    def _():
        for k0 in range(0, tb, batch):
            terms = [one(i * tb + k, k) for k in range(k0, k0 + batch)]
            for k, term in zip(range(k0, k0 + batch), terms):
                add(i * tb + k, term)

    @pl.when(jnp.logical_and(jnp.logical_not(full), i * tb < count))
    def _():
        def body(k, carry):
            t = i * tb + k

            @pl.when(t < count)
            def _():
                add(t, one(t, k))

            return carry

        lax.fori_loop(0, tb, body, 0)

    @pl.when(i == pl.num_programs(0) - 1)
    def _():
        own_ref[...] = acc_ref[:, :rows].T
        split = rows + ret_ref.shape[0]
        ret_ref[...] = acc_ref[:, rows:split].T.astype(ret_ref.dtype)
        hub_ref[...] = acc_ref[:, split:].T.astype(hub_ref.dtype)


def tile_backward_t(tile_src, tile_dst, tile_count, tile_val, daggT, src_rows, ret_rows, tb=16, batch=1):
    tiles, edge, _ = tile_val.shape
    width, rows = daggT.shape
    kernel = functools.partial(_back_kernel, tb=tb, edge=edge, batch=batch)
    return pl.pallas_call(
        kernel,
        out_shape=(
            jax.ShapeDtypeStruct((rows, width), jnp.float32),
            jax.ShapeDtypeStruct((ret_rows, width), jnp.bfloat16),
            jax.ShapeDtypeStruct((src_rows - rows - ret_rows, width), jnp.bfloat16),
        ),
        grid_spec=pltpu.PrefetchScalarGridSpec(
            num_scalar_prefetch=3, grid=(tiles // tb,),
            in_specs=[pl.BlockSpec((tb, edge, edge), _val_map(tb)),
                      pl.BlockSpec(daggT.shape, lambda i, s, d, c: (0, 0))],
            out_specs=[pl.BlockSpec((rows, width), lambda i, s, d, c: (0, 0)),
                       pl.BlockSpec((ret_rows, width), lambda i, s, d, c: (0, 0)),
                       pl.BlockSpec((src_rows - rows - ret_rows, width), lambda i, s, d, c: (0, 0))],
            scratch_shapes=[pltpu.VMEM((width, src_rows), jnp.float32)]),
        compiler_params=pltpu.CompilerParams(dimension_semantics=("arbitrary",)),
    )(tile_src, tile_dst, tile_count, tile_val, daggT)


def one_hot_rows(index, count):
    columns = lax.broadcasted_iota(jnp.int32, (index.shape[0], count), 1)
    return (columns == index[:, None]).astype(jnp.bfloat16)


def body(
    feats,
    w_self,
    w_neigh,
    cotangent,
    hub_rows,
    send_rows,
    send_count,
    tile_dst,
    tile_src,
    tile_count,
    tile_val,
):
    edge = tile_val.shape[1]
    rows, width = feats.shape
    peers = send_rows.shape[1]
    slots = send_rows.shape[2]
    group = lax.axis_size("dev")
    hubs_dev = hub_rows.shape[0]

    hub_pick = one_hot_rows(hub_rows, rows)
    own_hubs = jnp.dot(hub_pick, feats, preferred_element_type=jnp.float32).astype(jnp.bfloat16)
    hub_out = jnp.broadcast_to(own_hubs[None], (group, hubs_dev, width))
    hub_table = lax.all_to_all(hub_out, "dev", split_axis=0, concat_axis=0, tiled=True)
    hub_table = hub_table.reshape(group * hubs_dev, width)

    live = lax.broadcasted_iota(jnp.int32, (peers, slots), 1) < send_count[0][:, None]
    send_pick = one_hot_rows(send_rows[0].reshape(-1), rows)
    send_pick = jnp.where(live.reshape(-1, 1), send_pick, jnp.zeros((), jnp.bfloat16))
    outgoing = jnp.dot(send_pick, feats, preferred_element_type=jnp.float32).astype(jnp.bfloat16)
    outgoing = outgoing.reshape(peers, slots, width)
    incoming = lax.all_to_all(outgoing, ("dom", "dev"), split_axis=0, concat_axis=0, tiled=True)
    source = jnp.concatenate([feats, incoming.reshape(peers * slots, width), hub_table], axis=0)

    tb = _tile_block(tile_val.shape[0])
    agg = tile_aggregate(tile_src, tile_dst, tile_count, tile_val, source, rows, tb=tb)

    pre = jnp.dot(feats, w_self, preferred_element_type=jnp.float32) + jnp.dot(
        agg, w_neigh, preferred_element_type=jnp.float32
    )
    sig = jax.nn.sigmoid(pre)
    out = (pre * sig).astype(jnp.bfloat16)
    dpre = (cotangent.astype(jnp.float32) * sig * (1.0 + pre * (1.0 - sig))).astype(jnp.bfloat16)

    contract_rows = (((0,), (0,)), ((), ()))
    local_ws = lax.dot_general(feats, dpre, contract_rows, preferred_element_type=jnp.float32)
    local_wn = lax.dot_general(agg, dpre, contract_rows, preferred_element_type=jnp.float32)

    contract_cols = (((1,), (1,)), ((), ()))
    dagg_t = lax.dot_general(w_neigh, dpre, contract_cols, preferred_element_type=jnp.float32).astype(
        jnp.bfloat16
    )
    own, returning, hub_part = tile_backward_t(
        tile_src, tile_dst, tile_count, tile_val, dagg_t, source.shape[0], peers * slots, tb=tb
    )
    returning = returning.reshape(peers, slots, width)
    returned = lax.all_to_all(
        returning, ("dom", "dev"), split_axis=0, concat_axis=0, tiled=True
    )
    partial = jnp.concatenate([local_ws, local_wn], axis=0)
    hub_back = lax.all_to_all(
        hub_part.reshape(group, hubs_dev, width),
        "dev",
        split_axis=0,
        concat_axis=0,
        tiled=True,
    )
    partial, returned, hub_back = lax.optimization_barrier((partial, returned, hub_back))
    parts = partial.reshape(peers, -1, width)
    gathered = lax.all_to_all(parts, ("dom", "dev"), split_axis=0, concat_axis=0, tiled=True)
    scale = 1.0 / jnp.sqrt(jnp.float32(rows * peers))
    piece = (jnp.sum(gathered, axis=0) * scale).astype(jnp.bfloat16)
    spread_piece = jnp.broadcast_to(piece[None], (peers,) + piece.shape)
    summed = lax.all_to_all(spread_piece, ("dom", "dev"), split_axis=0, concat_axis=0, tiled=True)
    summed = summed.reshape(partial.shape).astype(jnp.float32)
    grad_ws = summed[: w_self.shape[0]]
    grad_wn = summed[w_self.shape[0] :]
    hub_spread = jnp.broadcast_to(hub_pick[None], (group,) + hub_pick.shape)
    grad = lax.dot_general(dpre, w_self, contract_cols, preferred_element_type=jnp.float32) + own
    grad = grad + lax.dot_general(
        send_pick, returned.reshape(peers * slots, width), contract_rows, preferred_element_type=jnp.float32
    )
    grad = grad + lax.dot_general(
        hub_spread.reshape(group * hubs_dev, rows),
        hub_back.reshape(group * hubs_dev, width),
        contract_rows,
        preferred_element_type=jnp.float32,
    )
    return (out, grad.astype(jnp.bfloat16), grad_ws, grad_wn)


def solution(mesh):
    return jax.shard_map(
        body,
        mesh=mesh,
        in_specs=(
            P(("dom", "dev"), None),
            P(),
            P(),
            P(("dom", "dev"), None),
            P(("dom", "dev")),
            P(("dom", "dev"), None, None),
            P(("dom", "dev"), None),
            P(("dom", "dev")),
            P(("dom", "dev")),
            P(("dom", "dev")),
            P(("dom", "dev"), None, None),
        ),
        out_specs=(P(("dom", "dev"), None), P(("dom", "dev"), None), P(), P()),
        check_vma=False,
    )
```

```python
import functools

import jax
import jax.numpy as jnp
from jax import lax
from jax.experimental import pallas as pl
from jax.experimental.pallas import tpu as pltpu
from jax.sharding import PartitionSpec as P


def _tile_block(tiles):
    for size in (80, 64, 40, 32, 16, 8, 4, 2, 1):
        if tiles % size == 0:
            return size
    return 1


def _val_map(tb):
    def index_map(i, src, dst, cnt):
        last = jnp.maximum(cnt[0] - 1, 0) // tb
        return (jnp.minimum(i, last), 0, 0)
    return index_map

def _agg_kernel(src_ref, dst_ref, cnt_ref, val_ref, source_ref, out_ref, acc_ref, *, tb, edge, batch):
    i = pl.program_id(0)
    last_src = source_ref.shape[0] // edge - 1
    last_dst = acc_ref.shape[0] // edge - 1
    @pl.when(i == 0)
    def _():
        acc_ref[...] = jnp.zeros_like(acc_ref)
    count = cnt_ref[0]
    def one(t, k):
        s = jnp.clip(src_ref[t], 0, last_src)
        x = source_ref[pl.ds(pl.multiple_of(s * edge, edge), edge), :]
        return jnp.dot(val_ref[k], x, preferred_element_type=jnp.float32)
    def add(t, term):
        d = jnp.clip(dst_ref[t], 0, last_dst)
        rows = pl.ds(pl.multiple_of(d * edge, edge), edge)
        acc_ref[rows, :] += term
    full = (i + 1) * tb <= count
    @pl.when(full)
    def _():
        for k0 in range(0, tb, batch):
            terms = [one(i * tb + k, k) for k in range(k0, k0 + batch)]
            for k, term in zip(range(k0, k0 + batch), terms):
                add(i * tb + k, term)
    @pl.when(jnp.logical_and(jnp.logical_not(full), i * tb < count))
    def _():
        def body(k, carry):
            t = i * tb + k
            @pl.when(t < count)
            def _():
                add(t, one(t, k))
            return carry
        lax.fori_loop(0, tb, body, 0)
    @pl.when(i == pl.num_programs(0) - 1)
    def _():
        out_ref[...] = acc_ref[...].astype(out_ref.dtype)

def tile_aggregate(tile_src, tile_dst, tile_count, tile_val, source, rows, tb=16, batch=1):
    tiles, edge, _ = tile_val.shape
    width = source.shape[1]
    kernel = functools.partial(_agg_kernel, tb=tb, edge=edge, batch=batch)
    return pl.pallas_call(
        kernel,
        out_shape=jax.ShapeDtypeStruct((rows, width), jnp.bfloat16),
        grid_spec=pltpu.PrefetchScalarGridSpec(
            num_scalar_prefetch=3, grid=(tiles // tb,),
            in_specs=[pl.BlockSpec((tb, edge, edge), _val_map(tb)),
                      pl.BlockSpec(source.shape, lambda i, s, d, c: (0, 0))],
            out_specs=pl.BlockSpec((rows, width), lambda i, s, d, c: (0, 0)),
            scratch_shapes=[pltpu.VMEM((rows, width), jnp.float32)]),
        compiler_params=pltpu.CompilerParams(dimension_semantics=("arbitrary",)),
    )(tile_src, tile_dst, tile_count, tile_val, source)

def _back_kernel(src_ref, dst_ref, cnt_ref, val_ref, dagg_ref, own_ref, ret_ref, hub_ref, acc_ref, *, tb, edge, batch):
    i = pl.program_id(0)
    last_src = acc_ref.shape[0] // edge - 1
    last_dst = dagg_ref.shape[0] // edge - 1
    rows = own_ref.shape[0]

    @pl.when(i == 0)
    def _():
        acc_ref[...] = jnp.zeros_like(acc_ref)

    count = cnt_ref[0]

    def one(t, k):
        d = jnp.clip(dst_ref[t], 0, last_dst)
        y = dagg_ref[pl.ds(pl.multiple_of(d * edge, edge), edge), :]
        return lax.dot_general(val_ref[k], y, (((0,), (0,)), ((), ())), preferred_element_type=jnp.float32)

    def add(t, term):
        s = jnp.clip(src_ref[t], 0, last_src)
        block = pl.ds(pl.multiple_of(s * edge, edge), edge)
        acc_ref[block, :] += term

    full = (i + 1) * tb <= count

    @pl.when(full)
    def _():
        for k0 in range(0, tb, batch):
            terms = [one(i * tb + k, k) for k in range(k0, k0 + batch)]
            for k, term in zip(range(k0, k0 + batch), terms):
                add(i * tb + k, term)

    @pl.when(jnp.logical_and(jnp.logical_not(full), i * tb < count))
    def _():
        def body(k, carry):
            t = i * tb + k

            @pl.when(t < count)
            def _():
                add(t, one(t, k))

            return carry

        lax.fori_loop(0, tb, body, 0)

    @pl.when(i == pl.num_programs(0) - 1)
    def _():
        split = rows + ret_ref.shape[0]
        own_ref[...] = acc_ref[:rows, :]
        ret_ref[...] = acc_ref[rows:split, :].astype(ret_ref.dtype)
        hub_ref[...] = acc_ref[split:, :].astype(hub_ref.dtype)


def tile_backward(tile_src, tile_dst, tile_count, tile_val, dagg, src_rows, ret_rows, tb=16, batch=1):
    tiles, edge, _ = tile_val.shape
    rows, width = dagg.shape
    kernel = functools.partial(_back_kernel, tb=tb, edge=edge, batch=batch)
    return pl.pallas_call(
        kernel,
        out_shape=(
            jax.ShapeDtypeStruct((rows, width), jnp.float32),
            jax.ShapeDtypeStruct((ret_rows, width), jnp.bfloat16),
            jax.ShapeDtypeStruct((src_rows - rows - ret_rows, width), jnp.bfloat16),
        ),
        grid_spec=pltpu.PrefetchScalarGridSpec(
            num_scalar_prefetch=3, grid=(tiles // tb,),
            in_specs=[pl.BlockSpec((tb, edge, edge), _val_map(tb)),
                      pl.BlockSpec(dagg.shape, lambda i, s, d, c: (0, 0))],
            out_specs=[pl.BlockSpec((rows, width), lambda i, s, d, c: (0, 0)),
                       pl.BlockSpec((ret_rows, width), lambda i, s, d, c: (0, 0)),
                       pl.BlockSpec((src_rows - rows - ret_rows, width), lambda i, s, d, c: (0, 0))],
            scratch_shapes=[pltpu.VMEM((src_rows, width), jnp.float32)]),
        compiler_params=pltpu.CompilerParams(dimension_semantics=("arbitrary",)),
    )(tile_src, tile_dst, tile_count, tile_val, dagg)


def one_hot_rows(index, count):
    columns = lax.broadcasted_iota(jnp.int32, (index.shape[0], count), 1)
    return (columns == index[:, None]).astype(jnp.bfloat16)


def body(
    feats,
    w_self,
    w_neigh,
    cotangent,
    hub_rows,
    send_rows,
    send_count,
    tile_dst,
    tile_src,
    tile_count,
    tile_val,
):
    edge = tile_val.shape[1]
    rows, width = feats.shape
    peers = send_rows.shape[1]
    slots = send_rows.shape[2]
    group = lax.axis_size("dev")
    hubs_dev = hub_rows.shape[0]

    hub_pick = one_hot_rows(hub_rows, rows)
    own_hubs = jnp.dot(hub_pick, feats, preferred_element_type=jnp.float32).astype(jnp.bfloat16)
    hub_out = jnp.broadcast_to(own_hubs[None], (group, hubs_dev, width))
    hub_table = lax.all_to_all(hub_out, "dev", split_axis=0, concat_axis=0, tiled=True)
    hub_table = hub_table.reshape(group * hubs_dev, width)

    live = lax.broadcasted_iota(jnp.int32, (peers, slots), 1) < send_count[0][:, None]
    send_pick = one_hot_rows(send_rows[0].reshape(-1), rows)
    send_pick = jnp.where(live.reshape(-1, 1), send_pick, jnp.zeros((), jnp.bfloat16))
    outgoing = jnp.dot(send_pick, feats, preferred_element_type=jnp.float32).astype(jnp.bfloat16)
    outgoing = outgoing.reshape(peers, slots, width)
    incoming = lax.all_to_all(outgoing, ("dom", "dev"), split_axis=0, concat_axis=0, tiled=True)
    source = jnp.concatenate([feats, incoming.reshape(peers * slots, width), hub_table], axis=0)

    tb = _tile_block(tile_val.shape[0])
    agg = tile_aggregate(tile_src, tile_dst, tile_count, tile_val, source, rows, tb=tb)

    pre = jnp.dot(feats, w_self, preferred_element_type=jnp.float32) + jnp.dot(
        agg, w_neigh, preferred_element_type=jnp.float32
    )
    sig = jax.nn.sigmoid(pre)
    out = (pre * sig).astype(jnp.bfloat16)
    dpre = (cotangent.astype(jnp.float32) * sig * (1.0 + pre * (1.0 - sig))).astype(jnp.bfloat16)

    contract_rows = (((0,), (0,)), ((), ()))
    local_ws = lax.dot_general(feats, dpre, contract_rows, preferred_element_type=jnp.float32)
    local_wn = lax.dot_general(agg, dpre, contract_rows, preferred_element_type=jnp.float32)

    contract_cols = (((1,), (1,)), ((), ()))
    dagg = lax.dot_general(dpre, w_neigh, contract_cols, preferred_element_type=jnp.float32).astype(
        jnp.bfloat16
    )
    own, returning, hub_part = tile_backward(
        tile_src, tile_dst, tile_count, tile_val, dagg, source.shape[0], peers * slots, tb=tb
    )
    returning = returning.reshape(peers, slots, width)
    returned = lax.all_to_all(
        returning, ("dom", "dev"), split_axis=0, concat_axis=0, tiled=True
    )
    partial = jnp.concatenate([local_ws, local_wn], axis=0)
    hub_back = lax.all_to_all(
        hub_part.reshape(group, hubs_dev, width),
        "dev",
        split_axis=0,
        concat_axis=0,
        tiled=True,
    )
    partial, returned, hub_back = lax.optimization_barrier((partial, returned, hub_back))
    parts = partial.reshape(peers, -1, width)
    gathered = lax.all_to_all(parts, ("dom", "dev"), split_axis=0, concat_axis=0, tiled=True)
    scale = 1.0 / jnp.sqrt(jnp.float32(rows * peers))
    piece = (jnp.sum(gathered, axis=0) * scale).astype(jnp.bfloat16)
    spread_piece = jnp.broadcast_to(piece[None], (peers,) + piece.shape)
    summed = lax.all_to_all(spread_piece, ("dom", "dev"), split_axis=0, concat_axis=0, tiled=True)
    summed = summed.reshape(partial.shape).astype(jnp.float32)
    grad_ws = summed[: w_self.shape[0]]
    grad_wn = summed[w_self.shape[0] :]
    hub_spread = jnp.broadcast_to(hub_pick[None], (group,) + hub_pick.shape)
    grad = lax.dot_general(dpre, w_self, contract_cols, preferred_element_type=jnp.float32) + own
    grad = grad + lax.dot_general(
        send_pick, returned.reshape(peers * slots, width), contract_rows, preferred_element_type=jnp.float32
    )
    grad = grad + lax.dot_general(
        hub_spread.reshape(group * hubs_dev, rows),
        hub_back.reshape(group * hubs_dev, width),
        contract_rows,
        preferred_element_type=jnp.float32,
    )
    return (out, grad.astype(jnp.bfloat16), grad_ws, grad_wn)


def solution(mesh):
    return jax.shard_map(
        body,
        mesh=mesh,
        in_specs=(
            P(("dom", "dev"), None),
            P(),
            P(),
            P(("dom", "dev"), None),
            P(("dom", "dev")),
            P(("dom", "dev"), None, None),
            P(("dom", "dev"), None),
            P(("dom", "dev")),
            P(("dom", "dev")),
            P(("dom", "dev")),
            P(("dom", "dev"), None, None),
        ),
        out_specs=(P(("dom", "dev"), None), P(("dom", "dev"), None), P(), P()),
        check_vma=False,
    )
```

```python
import functools

import jax
import jax.numpy as jnp
from jax import lax
from jax.experimental import pallas as pl
from jax.experimental.pallas import tpu as pltpu
from jax.sharding import PartitionSpec as P


def _tile_block(tiles):
    for size in (80, 64, 40, 32, 16, 8, 4, 2, 1):
        if tiles % size == 0:
            return size
    return 1


def _val_map(tb):
    def index_map(i, src, dst, cnt):
        last = jnp.maximum(cnt[0] - 1, 0) // tb
        return (jnp.minimum(i, last), 0, 0)
    return index_map

def _agg_kernel(src_ref, dst_ref, cnt_ref, val_ref, source_ref, out_ref, acc_ref, *, tb, edge, batch):
    i = pl.program_id(0)
    last_src = source_ref.shape[0] // edge - 1
    last_dst = acc_ref.shape[0] // edge - 1
    @pl.when(i == 0)
    def _():
        acc_ref[...] = jnp.zeros_like(acc_ref)
    count = cnt_ref[0]
    def one(t, k):
        s = jnp.clip(src_ref[t], 0, last_src)
        x = source_ref[pl.ds(pl.multiple_of(s * edge, edge), edge), :]
        return jnp.dot(val_ref[k], x, preferred_element_type=jnp.float32)
    def add(t, term):
        d = jnp.clip(dst_ref[t], 0, last_dst)
        rows = pl.ds(pl.multiple_of(d * edge, edge), edge)
        acc_ref[rows, :] += term
    full = (i + 1) * tb <= count
    @pl.when(full)
    def _():
        for k0 in range(0, tb, batch):
            terms = [one(i * tb + k, k) for k in range(k0, k0 + batch)]
            for k, term in zip(range(k0, k0 + batch), terms):
                add(i * tb + k, term)
    @pl.when(jnp.logical_and(jnp.logical_not(full), i * tb < count))
    def _():
        def body(k, carry):
            t = i * tb + k
            @pl.when(t < count)
            def _():
                add(t, one(t, k))
            return carry
        lax.fori_loop(0, tb, body, 0)
    @pl.when(i == pl.num_programs(0) - 1)
    def _():
        out_ref[...] = acc_ref[...].astype(out_ref.dtype)

def tile_aggregate(tile_src, tile_dst, tile_count, tile_val, source, rows, tb=16, batch=1):
    tiles, edge, _ = tile_val.shape
    width = source.shape[1]
    kernel = functools.partial(_agg_kernel, tb=tb, edge=edge, batch=batch)
    return pl.pallas_call(
        kernel,
        out_shape=jax.ShapeDtypeStruct((rows, width), jnp.bfloat16),
        grid_spec=pltpu.PrefetchScalarGridSpec(
            num_scalar_prefetch=3, grid=(tiles // tb,),
            in_specs=[pl.BlockSpec((tb, edge, edge), _val_map(tb)),
                      pl.BlockSpec(source.shape, lambda i, s, d, c: (0, 0))],
            out_specs=pl.BlockSpec((rows, width), lambda i, s, d, c: (0, 0)),
            scratch_shapes=[pltpu.VMEM((rows, width), jnp.float32)]),
        compiler_params=pltpu.CompilerParams(dimension_semantics=("arbitrary",)),
    )(tile_src, tile_dst, tile_count, tile_val, source)

def _back_kernel(src_ref, dst_ref, cnt_ref, val_ref, dagg_ref, own_ref, ret_ref, hub_ref, acc_ref, *, tb, edge, batch):
    i = pl.program_id(0)
    last_src = acc_ref.shape[0] // edge - 1
    last_dst = dagg_ref.shape[0] // edge - 1
    rows = own_ref.shape[0]

    @pl.when(i == 0)
    def _():
        acc_ref[...] = jnp.zeros_like(acc_ref)

    count = cnt_ref[0]

    def one(t, k):
        d = jnp.clip(dst_ref[t], 0, last_dst)
        y = dagg_ref[pl.ds(pl.multiple_of(d * edge, edge), edge), :]
        return lax.dot_general(val_ref[k], y, (((0,), (0,)), ((), ())), preferred_element_type=jnp.float32)

    def add(t, term):
        s = jnp.clip(src_ref[t], 0, last_src)
        block = pl.ds(pl.multiple_of(s * edge, edge), edge)
        acc_ref[block, :] += term

    full = (i + 1) * tb <= count

    @pl.when(full)
    def _():
        for k0 in range(0, tb, batch):
            terms = [one(i * tb + k, k) for k in range(k0, k0 + batch)]
            for k, term in zip(range(k0, k0 + batch), terms):
                add(i * tb + k, term)

    @pl.when(jnp.logical_and(jnp.logical_not(full), i * tb < count))
    def _():
        def body(k, carry):
            t = i * tb + k

            @pl.when(t < count)
            def _():
                add(t, one(t, k))

            return carry

        lax.fori_loop(0, tb, body, 0)

    @pl.when(i == pl.num_programs(0) - 1)
    def _():
        split = rows + ret_ref.shape[0]
        own_ref[...] = acc_ref[:rows, :]
        ret_ref[...] = acc_ref[rows:split, :].astype(ret_ref.dtype)
        hub_ref[...] = acc_ref[split:, :].astype(hub_ref.dtype)


def tile_backward(tile_src, tile_dst, tile_count, tile_val, dagg, src_rows, ret_rows, tb=16, batch=1):
    tiles, edge, _ = tile_val.shape
    rows, width = dagg.shape
    kernel = functools.partial(_back_kernel, tb=tb, edge=edge, batch=batch)
    return pl.pallas_call(
        kernel,
        out_shape=(
            jax.ShapeDtypeStruct((rows, width), jnp.float32),
            jax.ShapeDtypeStruct((ret_rows, width), jnp.bfloat16),
            jax.ShapeDtypeStruct((src_rows - rows - ret_rows, width), jnp.bfloat16),
        ),
        grid_spec=pltpu.PrefetchScalarGridSpec(
            num_scalar_prefetch=3, grid=(tiles // tb,),
            in_specs=[pl.BlockSpec((tb, edge, edge), _val_map(tb)),
                      pl.BlockSpec(dagg.shape, lambda i, s, d, c: (0, 0))],
            out_specs=[pl.BlockSpec((rows, width), lambda i, s, d, c: (0, 0)),
                       pl.BlockSpec((ret_rows, width), lambda i, s, d, c: (0, 0)),
                       pl.BlockSpec((src_rows - rows - ret_rows, width), lambda i, s, d, c: (0, 0))],
            scratch_shapes=[pltpu.VMEM((src_rows, width), jnp.float32)]),
        compiler_params=pltpu.CompilerParams(dimension_semantics=("arbitrary",)),
    )(tile_src, tile_dst, tile_count, tile_val, dagg)


def one_hot_rows(index, count):
    columns = lax.broadcasted_iota(jnp.int32, (index.shape[0], count), 1)
    return (columns == index[:, None]).astype(jnp.bfloat16)


def body(
    feats,
    w_self,
    w_neigh,
    cotangent,
    hub_rows,
    send_rows,
    send_count,
    tile_dst,
    tile_src,
    tile_count,
    tile_val,
):
    edge = tile_val.shape[1]
    rows, width = feats.shape
    peers = send_rows.shape[1]
    slots = send_rows.shape[2]
    group = lax.axis_size("dev")
    hubs_dev = hub_rows.shape[0]

    live = lax.broadcasted_iota(jnp.int32, (peers, slots), 1) < send_count[0][:, None]
    send_pick = one_hot_rows(send_rows[0].reshape(-1), rows)
    send_pick = jnp.where(live.reshape(-1, 1), send_pick, jnp.zeros((), jnp.bfloat16))
    outgoing = jnp.dot(send_pick, feats, preferred_element_type=jnp.float32).astype(jnp.bfloat16)
    outgoing = outgoing.reshape(peers, slots, width)
    incoming = lax.all_to_all(outgoing, ("dom", "dev"), split_axis=0, concat_axis=0, tiled=True)

    hub_pick = one_hot_rows(hub_rows, rows)
    own_hubs = jnp.dot(hub_pick, feats, preferred_element_type=jnp.float32).astype(jnp.bfloat16)
    hub_out = jnp.broadcast_to(own_hubs[None], (group, hubs_dev, width))
    hub_out, incoming = lax.optimization_barrier((hub_out, incoming))
    hub_table = lax.all_to_all(hub_out, "dev", split_axis=0, concat_axis=0, tiled=True)
    hub_table = hub_table.reshape(group * hubs_dev, width)
    source = jnp.concatenate([feats, incoming.reshape(peers * slots, width), hub_table], axis=0)

    tb = _tile_block(tile_val.shape[0])
    agg = tile_aggregate(tile_src, tile_dst, tile_count, tile_val, source, rows, tb=tb)

    pre = jnp.dot(feats, w_self, preferred_element_type=jnp.float32) + jnp.dot(
        agg, w_neigh, preferred_element_type=jnp.float32
    )
    sig = jax.nn.sigmoid(pre)
    out = (pre * sig).astype(jnp.bfloat16)
    dpre = (cotangent.astype(jnp.float32) * sig * (1.0 + pre * (1.0 - sig))).astype(jnp.bfloat16)

    contract_rows = (((0,), (0,)), ((), ()))
    local_ws = lax.dot_general(feats, dpre, contract_rows, preferred_element_type=jnp.float32)
    local_wn = lax.dot_general(agg, dpre, contract_rows, preferred_element_type=jnp.float32)

    contract_cols = (((1,), (1,)), ((), ()))
    dagg = lax.dot_general(dpre, w_neigh, contract_cols, preferred_element_type=jnp.float32).astype(
        jnp.bfloat16
    )
    own, returning, hub_part = tile_backward(
        tile_src, tile_dst, tile_count, tile_val, dagg, source.shape[0], peers * slots, tb=tb
    )
    returning = returning.reshape(peers, slots, width)
    returned = lax.all_to_all(
        returning, ("dom", "dev"), split_axis=0, concat_axis=0, tiled=True
    )
    partial = jnp.concatenate([local_ws, local_wn], axis=0)
    hub_back = lax.all_to_all(
        hub_part.reshape(group, hubs_dev, width),
        "dev",
        split_axis=0,
        concat_axis=0,
        tiled=True,
    )
    partial, returned, hub_back = lax.optimization_barrier((partial, returned, hub_back))
    parts = partial.reshape(peers, -1, width)
    gathered = lax.all_to_all(parts, ("dom", "dev"), split_axis=0, concat_axis=0, tiled=True)
    scale = 1.0 / jnp.sqrt(jnp.float32(rows * peers))
    piece = (jnp.sum(gathered, axis=0) * scale).astype(jnp.bfloat16)
    spread_piece = jnp.broadcast_to(piece[None], (peers,) + piece.shape)
    summed = lax.all_to_all(spread_piece, ("dom", "dev"), split_axis=0, concat_axis=0, tiled=True)
    summed = summed.reshape(partial.shape).astype(jnp.float32)
    grad_ws = summed[: w_self.shape[0]]
    grad_wn = summed[w_self.shape[0] :]
    hub_spread = jnp.broadcast_to(hub_pick[None], (group,) + hub_pick.shape)
    grad = lax.dot_general(dpre, w_self, contract_cols, preferred_element_type=jnp.float32) + own
    grad = grad + lax.dot_general(
        send_pick, returned.reshape(peers * slots, width), contract_rows, preferred_element_type=jnp.float32
    )
    grad = grad + lax.dot_general(
        hub_spread.reshape(group * hubs_dev, rows),
        hub_back.reshape(group * hubs_dev, width),
        contract_rows,
        preferred_element_type=jnp.float32,
    )
    return (out, grad.astype(jnp.bfloat16), grad_ws, grad_wn)


def solution(mesh):
    return jax.shard_map(
        body,
        mesh=mesh,
        in_specs=(
            P(("dom", "dev"), None),
            P(),
            P(),
            P(("dom", "dev"), None),
            P(("dom", "dev")),
            P(("dom", "dev"), None, None),
            P(("dom", "dev"), None),
            P(("dom", "dev")),
            P(("dom", "dev")),
            P(("dom", "dev")),
            P(("dom", "dev"), None, None),
        ),
        out_specs=(P(("dom", "dev"), None), P(("dom", "dev"), None), P(), P()),
        check_vma=False,
    )
```

```python
import functools

import jax
import jax.numpy as jnp
from jax import lax
from jax.experimental import pallas as pl
from jax.experimental.pallas import tpu as pltpu
from jax.sharding import PartitionSpec as P


def _tile_block(tiles):
    for size in (80, 64, 40, 32, 16, 8, 4, 2, 1):
        if tiles % size == 0:
            return size
    return 1


def _val_map(tb):
    def index_map(i, src, dst, cnt):
        last = jnp.maximum(cnt[0] - 1, 0) // tb
        return (jnp.minimum(i, last), 0, 0)
    return index_map

def _agg_kernel(src_ref, dst_ref, cnt_ref, val_ref, source_ref, fws_ref, wn_ref, cot_ref,
                agg_ref, out_ref, dpre_ref, dagg_ref, acc_ref, *, tb, edge, batch):
    i = pl.program_id(0)
    last_src = source_ref.shape[0] // edge - 1
    last_dst = acc_ref.shape[0] // edge - 1
    @pl.when(i == 0)
    def _():
        acc_ref[...] = jnp.zeros_like(acc_ref)
    count = cnt_ref[0]
    def one(t, k):
        s = jnp.clip(src_ref[t], 0, last_src)
        x = source_ref[pl.ds(pl.multiple_of(s * edge, edge), edge), :]
        return jnp.dot(val_ref[k], x, preferred_element_type=jnp.float32)
    def add(t, term):
        d = jnp.clip(dst_ref[t], 0, last_dst)
        rows = pl.ds(pl.multiple_of(d * edge, edge), edge)
        acc_ref[rows, :] += term
    full = (i + 1) * tb <= count
    @pl.when(full)
    def _():
        for k0 in range(0, tb, batch):
            terms = [one(i * tb + k, k) for k in range(k0, k0 + batch)]
            for k, term in zip(range(k0, k0 + batch), terms):
                add(i * tb + k, term)
    @pl.when(jnp.logical_and(jnp.logical_not(full), i * tb < count))
    def _():
        def body(k, carry):
            t = i * tb + k
            @pl.when(t < count)
            def _():
                add(t, one(t, k))
            return carry
        lax.fori_loop(0, tb, body, 0)
    @pl.when(i == pl.num_programs(0) - 1)
    def _():
        def rows_block(r, carry):
            blk = pl.ds(pl.multiple_of(r * edge, edge), edge)
            agg = acc_ref[blk, :].astype(jnp.bfloat16)
            agg_ref[blk, :] = agg
            pre = fws_ref[blk, :] + jnp.dot(agg, wn_ref[...], preferred_element_type=jnp.float32)
            sig = jax.nn.sigmoid(pre)
            out_ref[blk, :] = (pre * sig).astype(out_ref.dtype)
            cot = cot_ref[blk, :].astype(jnp.float32)
            dpre = (cot * sig * (1.0 + pre * (1.0 - sig))).astype(jnp.bfloat16)
            dpre_ref[blk, :] = dpre
            dagg = lax.dot_general(dpre, wn_ref[...], (((1,), (1,)), ((), ())), preferred_element_type=jnp.float32)
            dagg_ref[blk, :] = dagg.astype(dagg_ref.dtype)
            return carry

        lax.fori_loop(0, acc_ref.shape[0] // edge, rows_block, 0)

def tile_aggregate(tile_src, tile_dst, tile_count, tile_val, source, fws, w_neigh, cotangent, tb=16, batch=1):
    tiles, edge, _ = tile_val.shape
    rows, width = fws.shape
    kernel = functools.partial(_agg_kernel, tb=tb, edge=edge, batch=batch)
    whole = lambda i, s, d, c: (0, 0)
    row_out = jax.ShapeDtypeStruct((rows, width), jnp.bfloat16)
    return pl.pallas_call(
        kernel,
        out_shape=(row_out, row_out, row_out, row_out),
        grid_spec=pltpu.PrefetchScalarGridSpec(
            num_scalar_prefetch=3, grid=(tiles // tb,),
            in_specs=[pl.BlockSpec((tb, edge, edge), _val_map(tb)),
                      pl.BlockSpec(source.shape, whole),
                      pl.BlockSpec(fws.shape, whole),
                      pl.BlockSpec(w_neigh.shape, whole),
                      pl.BlockSpec(cotangent.shape, whole)],
            out_specs=[pl.BlockSpec((rows, width), whole) for _ in range(4)],
            scratch_shapes=[pltpu.VMEM((rows, width), jnp.float32)]),
        compiler_params=pltpu.CompilerParams(dimension_semantics=("arbitrary",)),
    )(tile_src, tile_dst, tile_count, tile_val, source, fws, w_neigh, cotangent)


def _back_kernel(src_ref, dst_ref, cnt_ref, val_ref, dagg_ref, own_ref, ret_ref, hub_ref, acc_ref, *, tb, edge, batch):
    i = pl.program_id(0)
    last_src = acc_ref.shape[0] // edge - 1
    last_dst = dagg_ref.shape[0] // edge - 1
    rows = own_ref.shape[0]

    @pl.when(i == 0)
    def _():
        acc_ref[...] = jnp.zeros_like(acc_ref)

    count = cnt_ref[0]

    def one(t, k):
        d = jnp.clip(dst_ref[t], 0, last_dst)
        y = dagg_ref[pl.ds(pl.multiple_of(d * edge, edge), edge), :]
        return lax.dot_general(val_ref[k], y, (((0,), (0,)), ((), ())), preferred_element_type=jnp.float32)

    def add(t, term):
        s = jnp.clip(src_ref[t], 0, last_src)
        block = pl.ds(pl.multiple_of(s * edge, edge), edge)
        acc_ref[block, :] += term

    full = (i + 1) * tb <= count

    @pl.when(full)
    def _():
        for k0 in range(0, tb, batch):
            terms = [one(i * tb + k, k) for k in range(k0, k0 + batch)]
            for k, term in zip(range(k0, k0 + batch), terms):
                add(i * tb + k, term)

    @pl.when(jnp.logical_and(jnp.logical_not(full), i * tb < count))
    def _():
        def body(k, carry):
            t = i * tb + k

            @pl.when(t < count)
            def _():
                add(t, one(t, k))

            return carry

        lax.fori_loop(0, tb, body, 0)

    @pl.when(i == pl.num_programs(0) - 1)
    def _():
        split = rows + ret_ref.shape[0]
        own_ref[...] = acc_ref[:rows, :]
        ret_ref[...] = acc_ref[rows:split, :].astype(ret_ref.dtype)
        hub_ref[...] = acc_ref[split:, :].astype(hub_ref.dtype)


def tile_backward(tile_src, tile_dst, tile_count, tile_val, dagg, src_rows, ret_rows, tb=16, batch=1):
    tiles, edge, _ = tile_val.shape
    rows, width = dagg.shape
    kernel = functools.partial(_back_kernel, tb=tb, edge=edge, batch=batch)
    return pl.pallas_call(
        kernel,
        out_shape=(
            jax.ShapeDtypeStruct((rows, width), jnp.float32),
            jax.ShapeDtypeStruct((ret_rows, width), jnp.bfloat16),
            jax.ShapeDtypeStruct((src_rows - rows - ret_rows, width), jnp.bfloat16),
        ),
        grid_spec=pltpu.PrefetchScalarGridSpec(
            num_scalar_prefetch=3, grid=(tiles // tb,),
            in_specs=[pl.BlockSpec((tb, edge, edge), _val_map(tb)),
                      pl.BlockSpec(dagg.shape, lambda i, s, d, c: (0, 0))],
            out_specs=[pl.BlockSpec((rows, width), lambda i, s, d, c: (0, 0)),
                       pl.BlockSpec((ret_rows, width), lambda i, s, d, c: (0, 0)),
                       pl.BlockSpec((src_rows - rows - ret_rows, width), lambda i, s, d, c: (0, 0))],
            scratch_shapes=[pltpu.VMEM((src_rows, width), jnp.float32)]),
        compiler_params=pltpu.CompilerParams(dimension_semantics=("arbitrary",)),
    )(tile_src, tile_dst, tile_count, tile_val, dagg)


def one_hot_rows(index, count):
    columns = lax.broadcasted_iota(jnp.int32, (index.shape[0], count), 1)
    return (columns == index[:, None]).astype(jnp.bfloat16)


def body(
    feats,
    w_self,
    w_neigh,
    cotangent,
    hub_rows,
    send_rows,
    send_count,
    tile_dst,
    tile_src,
    tile_count,
    tile_val,
):
    edge = tile_val.shape[1]
    rows, width = feats.shape
    peers = send_rows.shape[1]
    slots = send_rows.shape[2]
    group = lax.axis_size("dev")
    hubs_dev = hub_rows.shape[0]

    hub_pick = one_hot_rows(hub_rows, rows)
    own_hubs = jnp.dot(hub_pick, feats, preferred_element_type=jnp.float32).astype(jnp.bfloat16)
    hub_out = jnp.broadcast_to(own_hubs[None], (group, hubs_dev, width))
    hub_table = lax.all_to_all(hub_out, "dev", split_axis=0, concat_axis=0, tiled=True)
    hub_table = hub_table.reshape(group * hubs_dev, width)

    live = lax.broadcasted_iota(jnp.int32, (peers, slots), 1) < send_count[0][:, None]
    send_pick = one_hot_rows(send_rows[0].reshape(-1), rows)
    send_pick = jnp.where(live.reshape(-1, 1), send_pick, jnp.zeros((), jnp.bfloat16))
    outgoing = jnp.dot(send_pick, feats, preferred_element_type=jnp.float32).astype(jnp.bfloat16)
    outgoing = outgoing.reshape(peers, slots, width)
    incoming = lax.all_to_all(outgoing, ("dom", "dev"), split_axis=0, concat_axis=0, tiled=True)
    source = jnp.concatenate([feats, incoming.reshape(peers * slots, width), hub_table], axis=0)

    tb = _tile_block(tile_val.shape[0])
    fws = jnp.dot(feats, w_self, preferred_element_type=jnp.float32)
    agg, out, dpre, dagg = tile_aggregate(
        tile_src, tile_dst, tile_count, tile_val, source, fws, w_neigh, cotangent, tb=tb
    )

    contract_rows = (((0,), (0,)), ((), ()))
    local_ws = lax.dot_general(feats, dpre, contract_rows, preferred_element_type=jnp.float32)
    local_wn = lax.dot_general(agg, dpre, contract_rows, preferred_element_type=jnp.float32)

    contract_cols = (((1,), (1,)), ((), ()))
    own, returning, hub_part = tile_backward(
        tile_src, tile_dst, tile_count, tile_val, dagg, source.shape[0], peers * slots, tb=tb
    )
    returning = returning.reshape(peers, slots, width)
    returned = lax.all_to_all(
        returning, ("dom", "dev"), split_axis=0, concat_axis=0, tiled=True
    )
    partial = jnp.concatenate([local_ws, local_wn], axis=0)
    hub_back = lax.all_to_all(
        hub_part.reshape(group, hubs_dev, width),
        "dev",
        split_axis=0,
        concat_axis=0,
        tiled=True,
    )
    partial, returned, hub_back = lax.optimization_barrier((partial, returned, hub_back))
    parts = partial.reshape(peers, -1, width)
    gathered = lax.all_to_all(parts, ("dom", "dev"), split_axis=0, concat_axis=0, tiled=True)
    scale = 1.0 / jnp.sqrt(jnp.float32(rows * peers))
    piece = (jnp.sum(gathered, axis=0) * scale).astype(jnp.bfloat16)
    spread_piece = jnp.broadcast_to(piece[None], (peers,) + piece.shape)
    summed = lax.all_to_all(spread_piece, ("dom", "dev"), split_axis=0, concat_axis=0, tiled=True)
    summed = summed.reshape(partial.shape).astype(jnp.float32)
    grad_ws = summed[: w_self.shape[0]]
    grad_wn = summed[w_self.shape[0] :]
    hub_spread = jnp.broadcast_to(hub_pick[None], (group,) + hub_pick.shape)
    grad = lax.dot_general(dpre, w_self, contract_cols, preferred_element_type=jnp.float32) + own
    grad = grad + lax.dot_general(
        send_pick, returned.reshape(peers * slots, width), contract_rows, preferred_element_type=jnp.float32
    )
    grad = grad + lax.dot_general(
        hub_spread.reshape(group * hubs_dev, rows),
        hub_back.reshape(group * hubs_dev, width),
        contract_rows,
        preferred_element_type=jnp.float32,
    )
    return (out, grad.astype(jnp.bfloat16), grad_ws, grad_wn)


def solution(mesh):
    return jax.shard_map(
        body,
        mesh=mesh,
        in_specs=(
            P(("dom", "dev"), None),
            P(),
            P(),
            P(("dom", "dev"), None),
            P(("dom", "dev")),
            P(("dom", "dev"), None, None),
            P(("dom", "dev"), None),
            P(("dom", "dev")),
            P(("dom", "dev")),
            P(("dom", "dev")),
            P(("dom", "dev"), None, None),
        ),
        out_specs=(P(("dom", "dev"), None), P(("dom", "dev"), None), P(), P()),
        check_vma=False,
    )
```

```python
import functools

import jax
import jax.numpy as jnp
from jax import lax
from jax.experimental import pallas as pl
from jax.experimental.pallas import tpu as pltpu
from jax.sharding import PartitionSpec as P


def _tile_block(tiles):
    for size in (80, 64, 40, 32, 16, 8, 4, 2, 1):
        if tiles % size == 0:
            return size
    return 1


def _val_map(tb):
    def index_map(i, src, dst, cnt):
        last = jnp.maximum(cnt[0] - 1, 0) // tb
        return (jnp.minimum(i, last), 0, 0)
    return index_map

def _agg_kernel(src_ref, dst_ref, cnt_ref, val_ref, source_ref, fws_ref, wn_ref, cot_ref,
                agg_ref, out_ref, dpre_ref, dagg_ref, acc_ref, *, tb, edge, batch):
    i = pl.program_id(0)
    last_src = source_ref.shape[0] // edge - 1
    last_dst = acc_ref.shape[0] // edge - 1
    @pl.when(i == 0)
    def _():
        acc_ref[...] = jnp.zeros_like(acc_ref)
    count = cnt_ref[0]
    def one(t, k):
        s = jnp.clip(src_ref[t], 0, last_src)
        x = source_ref[pl.ds(pl.multiple_of(s * edge, edge), edge), :]
        return jnp.dot(val_ref[k], x, preferred_element_type=jnp.float32)
    def add(t, term):
        d = jnp.clip(dst_ref[t], 0, last_dst)
        rows = pl.ds(pl.multiple_of(d * edge, edge), edge)
        acc_ref[rows, :] += term
    full = (i + 1) * tb <= count
    @pl.when(full)
    def _():
        for k0 in range(0, tb, batch):
            terms = [one(i * tb + k, k) for k in range(k0, k0 + batch)]
            for k, term in zip(range(k0, k0 + batch), terms):
                add(i * tb + k, term)
    @pl.when(jnp.logical_and(jnp.logical_not(full), i * tb < count))
    def _():
        def body(k, carry):
            t = i * tb + k
            @pl.when(t < count)
            def _():
                add(t, one(t, k))
            return carry
        lax.fori_loop(0, tb, body, 0)
    @pl.when(i == pl.num_programs(0) - 1)
    def _():
        def rows_block(r, carry):
            blk = pl.ds(pl.multiple_of(r * edge, edge), edge)
            agg = acc_ref[blk, :].astype(jnp.bfloat16)
            agg_ref[blk, :] = agg
            pre = fws_ref[blk, :] + jnp.dot(agg, wn_ref[...], preferred_element_type=jnp.float32)
            sig = jax.nn.sigmoid(pre)
            out_ref[blk, :] = (pre * sig).astype(out_ref.dtype)
            cot = cot_ref[blk, :].astype(jnp.float32)
            dpre = (cot * sig * (1.0 + pre * (1.0 - sig))).astype(jnp.bfloat16)
            dpre_ref[blk, :] = dpre
            dagg = lax.dot_general(dpre, wn_ref[...], (((1,), (1,)), ((), ())), preferred_element_type=jnp.float32)
            dagg_ref[blk, :] = dagg.astype(dagg_ref.dtype)
            return carry

        lax.fori_loop(0, acc_ref.shape[0] // edge, rows_block, 0, unroll=True)

def tile_aggregate(tile_src, tile_dst, tile_count, tile_val, source, fws, w_neigh, cotangent, tb=16, batch=1):
    tiles, edge, _ = tile_val.shape
    rows, width = fws.shape
    kernel = functools.partial(_agg_kernel, tb=tb, edge=edge, batch=batch)
    whole = lambda i, s, d, c: (0, 0)
    row_out = jax.ShapeDtypeStruct((rows, width), jnp.bfloat16)
    return pl.pallas_call(
        kernel,
        out_shape=(row_out, row_out, row_out, row_out),
        grid_spec=pltpu.PrefetchScalarGridSpec(
            num_scalar_prefetch=3, grid=(tiles // tb,),
            in_specs=[pl.BlockSpec((tb, edge, edge), _val_map(tb)),
                      pl.BlockSpec(source.shape, whole),
                      pl.BlockSpec(fws.shape, whole),
                      pl.BlockSpec(w_neigh.shape, whole),
                      pl.BlockSpec(cotangent.shape, whole)],
            out_specs=[pl.BlockSpec((rows, width), whole) for _ in range(4)],
            scratch_shapes=[pltpu.VMEM((rows, width), jnp.float32)]),
        compiler_params=pltpu.CompilerParams(dimension_semantics=("arbitrary",)),
    )(tile_src, tile_dst, tile_count, tile_val, source, fws, w_neigh, cotangent)


def _back_kernel(src_ref, dst_ref, cnt_ref, val_ref, dagg_ref, own_ref, ret_ref, hub_ref, acc_ref, *, tb, edge, batch):
    i = pl.program_id(0)
    last_src = acc_ref.shape[0] // edge - 1
    last_dst = dagg_ref.shape[0] // edge - 1
    rows = own_ref.shape[0]

    @pl.when(i == 0)
    def _():
        acc_ref[...] = jnp.zeros_like(acc_ref)

    count = cnt_ref[0]

    def one(t, k):
        d = jnp.clip(dst_ref[t], 0, last_dst)
        y = dagg_ref[pl.ds(pl.multiple_of(d * edge, edge), edge), :]
        return lax.dot_general(val_ref[k], y, (((0,), (0,)), ((), ())), preferred_element_type=jnp.float32)

    def add(t, term):
        s = jnp.clip(src_ref[t], 0, last_src)
        block = pl.ds(pl.multiple_of(s * edge, edge), edge)
        acc_ref[block, :] += term

    full = (i + 1) * tb <= count

    @pl.when(full)
    def _():
        for k0 in range(0, tb, batch):
            terms = [one(i * tb + k, k) for k in range(k0, k0 + batch)]
            for k, term in zip(range(k0, k0 + batch), terms):
                add(i * tb + k, term)

    @pl.when(jnp.logical_and(jnp.logical_not(full), i * tb < count))
    def _():
        def body(k, carry):
            t = i * tb + k

            @pl.when(t < count)
            def _():
                add(t, one(t, k))

            return carry

        lax.fori_loop(0, tb, body, 0)

    @pl.when(i == pl.num_programs(0) - 1)
    def _():
        split = rows + ret_ref.shape[0]
        own_ref[...] = acc_ref[:rows, :]
        ret_ref[...] = acc_ref[rows:split, :].astype(ret_ref.dtype)
        hub_ref[...] = acc_ref[split:, :].astype(hub_ref.dtype)


def tile_backward(tile_src, tile_dst, tile_count, tile_val, dagg, src_rows, ret_rows, tb=16, batch=1):
    tiles, edge, _ = tile_val.shape
    rows, width = dagg.shape
    kernel = functools.partial(_back_kernel, tb=tb, edge=edge, batch=batch)
    return pl.pallas_call(
        kernel,
        out_shape=(
            jax.ShapeDtypeStruct((rows, width), jnp.float32),
            jax.ShapeDtypeStruct((ret_rows, width), jnp.bfloat16),
            jax.ShapeDtypeStruct((src_rows - rows - ret_rows, width), jnp.bfloat16),
        ),
        grid_spec=pltpu.PrefetchScalarGridSpec(
            num_scalar_prefetch=3, grid=(tiles // tb,),
            in_specs=[pl.BlockSpec((tb, edge, edge), _val_map(tb)),
                      pl.BlockSpec(dagg.shape, lambda i, s, d, c: (0, 0))],
            out_specs=[pl.BlockSpec((rows, width), lambda i, s, d, c: (0, 0)),
                       pl.BlockSpec((ret_rows, width), lambda i, s, d, c: (0, 0)),
                       pl.BlockSpec((src_rows - rows - ret_rows, width), lambda i, s, d, c: (0, 0))],
            scratch_shapes=[pltpu.VMEM((src_rows, width), jnp.float32)]),
        compiler_params=pltpu.CompilerParams(dimension_semantics=("arbitrary",)),
    )(tile_src, tile_dst, tile_count, tile_val, dagg)


def one_hot_rows(index, count):
    columns = lax.broadcasted_iota(jnp.int32, (index.shape[0], count), 1)
    return (columns == index[:, None]).astype(jnp.bfloat16)


def body(
    feats,
    w_self,
    w_neigh,
    cotangent,
    hub_rows,
    send_rows,
    send_count,
    tile_dst,
    tile_src,
    tile_count,
    tile_val,
):
    edge = tile_val.shape[1]
    rows, width = feats.shape
    peers = send_rows.shape[1]
    slots = send_rows.shape[2]
    group = lax.axis_size("dev")
    hubs_dev = hub_rows.shape[0]

    hub_pick = one_hot_rows(hub_rows, rows)
    own_hubs = jnp.dot(hub_pick, feats, preferred_element_type=jnp.float32).astype(jnp.bfloat16)
    hub_out = jnp.broadcast_to(own_hubs[None], (group, hubs_dev, width))
    hub_table = lax.all_to_all(hub_out, "dev", split_axis=0, concat_axis=0, tiled=True)
    hub_table = hub_table.reshape(group * hubs_dev, width)

    live = lax.broadcasted_iota(jnp.int32, (peers, slots), 1) < send_count[0][:, None]
    send_pick = one_hot_rows(send_rows[0].reshape(-1), rows)
    send_pick = jnp.where(live.reshape(-1, 1), send_pick, jnp.zeros((), jnp.bfloat16))
    outgoing = jnp.dot(send_pick, feats, preferred_element_type=jnp.float32).astype(jnp.bfloat16)
    outgoing = outgoing.reshape(peers, slots, width)
    incoming = lax.all_to_all(outgoing, ("dom", "dev"), split_axis=0, concat_axis=0, tiled=True)
    source = jnp.concatenate([feats, incoming.reshape(peers * slots, width), hub_table], axis=0)

    tb = _tile_block(tile_val.shape[0])
    fws = jnp.dot(feats, w_self, preferred_element_type=jnp.float32)
    agg, out, dpre, dagg = tile_aggregate(
        tile_src, tile_dst, tile_count, tile_val, source, fws, w_neigh, cotangent, tb=tb
    )

    contract_rows = (((0,), (0,)), ((), ()))
    local_ws = lax.dot_general(feats, dpre, contract_rows, preferred_element_type=jnp.float32)
    local_wn = lax.dot_general(agg, dpre, contract_rows, preferred_element_type=jnp.float32)

    contract_cols = (((1,), (1,)), ((), ()))
    own, returning, hub_part = tile_backward(
        tile_src, tile_dst, tile_count, tile_val, dagg, source.shape[0], peers * slots, tb=tb
    )
    returning = returning.reshape(peers, slots, width)
    returned = lax.all_to_all(
        returning, ("dom", "dev"), split_axis=0, concat_axis=0, tiled=True
    )
    partial = jnp.concatenate([local_ws, local_wn], axis=0)
    hub_back = lax.all_to_all(
        hub_part.reshape(group, hubs_dev, width),
        "dev",
        split_axis=0,
        concat_axis=0,
        tiled=True,
    )
    partial, returned, hub_back = lax.optimization_barrier((partial, returned, hub_back))
    parts = partial.reshape(peers, -1, width)
    gathered = lax.all_to_all(parts, ("dom", "dev"), split_axis=0, concat_axis=0, tiled=True)
    scale = 1.0 / jnp.sqrt(jnp.float32(rows * peers))
    piece = (jnp.sum(gathered, axis=0) * scale).astype(jnp.bfloat16)
    spread_piece = jnp.broadcast_to(piece[None], (peers,) + piece.shape)
    summed = lax.all_to_all(spread_piece, ("dom", "dev"), split_axis=0, concat_axis=0, tiled=True)
    summed = summed.reshape(partial.shape).astype(jnp.float32)
    grad_ws = summed[: w_self.shape[0]]
    grad_wn = summed[w_self.shape[0] :]
    hub_spread = jnp.broadcast_to(hub_pick[None], (group,) + hub_pick.shape)
    grad = lax.dot_general(dpre, w_self, contract_cols, preferred_element_type=jnp.float32) + own
    grad = grad + lax.dot_general(
        send_pick, returned.reshape(peers * slots, width), contract_rows, preferred_element_type=jnp.float32
    )
    grad = grad + lax.dot_general(
        hub_spread.reshape(group * hubs_dev, rows),
        hub_back.reshape(group * hubs_dev, width),
        contract_rows,
        preferred_element_type=jnp.float32,
    )
    return (out, grad.astype(jnp.bfloat16), grad_ws, grad_wn)


def solution(mesh):
    return jax.shard_map(
        body,
        mesh=mesh,
        in_specs=(
            P(("dom", "dev"), None),
            P(),
            P(),
            P(("dom", "dev"), None),
            P(("dom", "dev")),
            P(("dom", "dev"), None, None),
            P(("dom", "dev"), None),
            P(("dom", "dev")),
            P(("dom", "dev")),
            P(("dom", "dev")),
            P(("dom", "dev"), None, None),
        ),
        out_specs=(P(("dom", "dev"), None), P(("dom", "dev"), None), P(), P()),
        check_vma=False,
    )
```

```python
import functools

import jax
import jax.numpy as jnp
from jax import lax
from jax.experimental import pallas as pl
from jax.experimental.pallas import tpu as pltpu
from jax.sharding import PartitionSpec as P


def _tile_block(tiles):
    for size in (80, 64, 40, 32, 16, 8, 4, 2, 1):
        if tiles % size == 0:
            return size
    return 1


def _val_map(tb):
    def index_map(i, src, dst, cnt):
        last = jnp.maximum(cnt[0] - 1, 0) // tb
        return (jnp.minimum(i, last), 0, 0)
    return index_map

def _agg_kernel(src_ref, dst_ref, cnt_ref, val_ref, feats_ref, inc_ref, hub_ref, out_ref, acc_ref, source_ref, *, tb, edge, batch):
    i = pl.program_id(0)
    last_src = source_ref.shape[0] // edge - 1
    last_dst = acc_ref.shape[0] // edge - 1
    @pl.when(i == 0)
    def _():
        acc_ref[...] = jnp.zeros_like(acc_ref)
        own = feats_ref.shape[0]
        mid = own + inc_ref.shape[0]
        source_ref[:own, :] = feats_ref[...]
        source_ref[own:mid, :] = inc_ref[...]
        source_ref[mid:, :] = hub_ref[...]
    count = cnt_ref[0]
    def one(t, k):
        s = jnp.clip(src_ref[t], 0, last_src)
        x = source_ref[pl.ds(pl.multiple_of(s * edge, edge), edge), :]
        return jnp.dot(val_ref[k], x, preferred_element_type=jnp.float32)
    def add(t, term):
        d = jnp.clip(dst_ref[t], 0, last_dst)
        rows = pl.ds(pl.multiple_of(d * edge, edge), edge)
        acc_ref[rows, :] += term
    full = (i + 1) * tb <= count
    @pl.when(full)
    def _():
        for k0 in range(0, tb, batch):
            terms = [one(i * tb + k, k) for k in range(k0, k0 + batch)]
            for k, term in zip(range(k0, k0 + batch), terms):
                add(i * tb + k, term)
    @pl.when(jnp.logical_and(jnp.logical_not(full), i * tb < count))
    def _():
        def body(k, carry):
            t = i * tb + k
            @pl.when(t < count)
            def _():
                add(t, one(t, k))
            return carry
        lax.fori_loop(0, tb, body, 0)
    @pl.when(i == pl.num_programs(0) - 1)
    def _():
        out_ref[...] = acc_ref[...].astype(out_ref.dtype)

def tile_aggregate(tile_src, tile_dst, tile_count, tile_val, feats, incoming, hub_table, tb=16, batch=1):
    tiles, edge, _ = tile_val.shape
    rows, width = feats.shape
    src_rows = rows + incoming.shape[0] + hub_table.shape[0]
    kernel = functools.partial(_agg_kernel, tb=tb, edge=edge, batch=batch)
    whole = lambda i, s, d, c: (0, 0)
    return pl.pallas_call(
        kernel,
        out_shape=jax.ShapeDtypeStruct((rows, width), jnp.bfloat16),
        grid_spec=pltpu.PrefetchScalarGridSpec(
            num_scalar_prefetch=3, grid=(tiles // tb,),
            in_specs=[pl.BlockSpec((tb, edge, edge), _val_map(tb)),
                      pl.BlockSpec(feats.shape, whole),
                      pl.BlockSpec(incoming.shape, whole),
                      pl.BlockSpec(hub_table.shape, whole)],
            out_specs=pl.BlockSpec((rows, width), whole),
            scratch_shapes=[pltpu.VMEM((rows, width), jnp.float32),
                            pltpu.VMEM((src_rows, width), feats.dtype)]),
        compiler_params=pltpu.CompilerParams(dimension_semantics=("arbitrary",)),
    )(tile_src, tile_dst, tile_count, tile_val, feats, incoming, hub_table)


def _back_kernel(src_ref, dst_ref, cnt_ref, val_ref, dagg_ref, own_ref, ret_ref, hub_ref, acc_ref, *, tb, edge, batch):
    i = pl.program_id(0)
    last_src = acc_ref.shape[0] // edge - 1
    last_dst = dagg_ref.shape[0] // edge - 1
    rows = own_ref.shape[0]

    @pl.when(i == 0)
    def _():
        acc_ref[...] = jnp.zeros_like(acc_ref)

    count = cnt_ref[0]

    def one(t, k):
        d = jnp.clip(dst_ref[t], 0, last_dst)
        y = dagg_ref[pl.ds(pl.multiple_of(d * edge, edge), edge), :]
        return lax.dot_general(val_ref[k], y, (((0,), (0,)), ((), ())), preferred_element_type=jnp.float32)

    def add(t, term):
        s = jnp.clip(src_ref[t], 0, last_src)
        block = pl.ds(pl.multiple_of(s * edge, edge), edge)
        acc_ref[block, :] += term

    full = (i + 1) * tb <= count

    @pl.when(full)
    def _():
        for k0 in range(0, tb, batch):
            terms = [one(i * tb + k, k) for k in range(k0, k0 + batch)]
            for k, term in zip(range(k0, k0 + batch), terms):
                add(i * tb + k, term)

    @pl.when(jnp.logical_and(jnp.logical_not(full), i * tb < count))
    def _():
        def body(k, carry):
            t = i * tb + k

            @pl.when(t < count)
            def _():
                add(t, one(t, k))

            return carry

        lax.fori_loop(0, tb, body, 0)

    @pl.when(i == pl.num_programs(0) - 1)
    def _():
        split = rows + ret_ref.shape[0]
        own_ref[...] = acc_ref[:rows, :]
        ret_ref[...] = acc_ref[rows:split, :].astype(ret_ref.dtype)
        hub_ref[...] = acc_ref[split:, :].astype(hub_ref.dtype)


def tile_backward(tile_src, tile_dst, tile_count, tile_val, dagg, src_rows, ret_rows, tb=16, batch=1):
    tiles, edge, _ = tile_val.shape
    rows, width = dagg.shape
    kernel = functools.partial(_back_kernel, tb=tb, edge=edge, batch=batch)
    return pl.pallas_call(
        kernel,
        out_shape=(
            jax.ShapeDtypeStruct((rows, width), jnp.float32),
            jax.ShapeDtypeStruct((ret_rows, width), jnp.bfloat16),
            jax.ShapeDtypeStruct((src_rows - rows - ret_rows, width), jnp.bfloat16),
        ),
        grid_spec=pltpu.PrefetchScalarGridSpec(
            num_scalar_prefetch=3, grid=(tiles // tb,),
            in_specs=[pl.BlockSpec((tb, edge, edge), _val_map(tb)),
                      pl.BlockSpec(dagg.shape, lambda i, s, d, c: (0, 0))],
            out_specs=[pl.BlockSpec((rows, width), lambda i, s, d, c: (0, 0)),
                       pl.BlockSpec((ret_rows, width), lambda i, s, d, c: (0, 0)),
                       pl.BlockSpec((src_rows - rows - ret_rows, width), lambda i, s, d, c: (0, 0))],
            scratch_shapes=[pltpu.VMEM((src_rows, width), jnp.float32)]),
        compiler_params=pltpu.CompilerParams(dimension_semantics=("arbitrary",)),
    )(tile_src, tile_dst, tile_count, tile_val, dagg)


def one_hot_rows(index, count):
    columns = lax.broadcasted_iota(jnp.int32, (index.shape[0], count), 1)
    return (columns == index[:, None]).astype(jnp.bfloat16)


def body(
    feats,
    w_self,
    w_neigh,
    cotangent,
    hub_rows,
    send_rows,
    send_count,
    tile_dst,
    tile_src,
    tile_count,
    tile_val,
):
    edge = tile_val.shape[1]
    rows, width = feats.shape
    peers = send_rows.shape[1]
    slots = send_rows.shape[2]
    group = lax.axis_size("dev")
    hubs_dev = hub_rows.shape[0]

    hub_pick = one_hot_rows(hub_rows, rows)
    own_hubs = jnp.dot(hub_pick, feats, preferred_element_type=jnp.float32).astype(jnp.bfloat16)
    hub_out = jnp.broadcast_to(own_hubs[None], (group, hubs_dev, width))
    hub_table = lax.all_to_all(hub_out, "dev", split_axis=0, concat_axis=0, tiled=True)
    hub_table = hub_table.reshape(group * hubs_dev, width)

    live = lax.broadcasted_iota(jnp.int32, (peers, slots), 1) < send_count[0][:, None]
    send_pick = one_hot_rows(send_rows[0].reshape(-1), rows)
    send_pick = jnp.where(live.reshape(-1, 1), send_pick, jnp.zeros((), jnp.bfloat16))
    outgoing = jnp.dot(send_pick, feats, preferred_element_type=jnp.float32).astype(jnp.bfloat16)
    outgoing = outgoing.reshape(peers, slots, width)
    incoming = lax.all_to_all(outgoing, ("dom", "dev"), split_axis=0, concat_axis=0, tiled=True)
    incoming = incoming.reshape(peers * slots, width)
    src_rows = rows + incoming.shape[0] + hub_table.shape[0]

    tb = _tile_block(tile_val.shape[0])
    agg = tile_aggregate(tile_src, tile_dst, tile_count, tile_val, feats, incoming, hub_table, tb=tb)

    pre = jnp.dot(feats, w_self, preferred_element_type=jnp.float32) + jnp.dot(
        agg, w_neigh, preferred_element_type=jnp.float32
    )
    sig = jax.nn.sigmoid(pre)
    out = (pre * sig).astype(jnp.bfloat16)
    dpre = (cotangent.astype(jnp.float32) * sig * (1.0 + pre * (1.0 - sig))).astype(jnp.bfloat16)

    contract_rows = (((0,), (0,)), ((), ()))
    local_ws = lax.dot_general(feats, dpre, contract_rows, preferred_element_type=jnp.float32)
    local_wn = lax.dot_general(agg, dpre, contract_rows, preferred_element_type=jnp.float32)

    contract_cols = (((1,), (1,)), ((), ()))
    dagg = lax.dot_general(dpre, w_neigh, contract_cols, preferred_element_type=jnp.float32).astype(
        jnp.bfloat16
    )
    own, returning, hub_part = tile_backward(
        tile_src, tile_dst, tile_count, tile_val, dagg, src_rows, peers * slots, tb=tb
    )
    returning = returning.reshape(peers, slots, width)
    returned = lax.all_to_all(
        returning, ("dom", "dev"), split_axis=0, concat_axis=0, tiled=True
    )
    partial = jnp.concatenate([local_ws, local_wn], axis=0)
    hub_back = lax.all_to_all(
        hub_part.reshape(group, hubs_dev, width),
        "dev",
        split_axis=0,
        concat_axis=0,
        tiled=True,
    )
    partial, returned, hub_back = lax.optimization_barrier((partial, returned, hub_back))
    parts = partial.reshape(peers, -1, width)
    gathered = lax.all_to_all(parts, ("dom", "dev"), split_axis=0, concat_axis=0, tiled=True)
    scale = 1.0 / jnp.sqrt(jnp.float32(rows * peers))
    piece = (jnp.sum(gathered, axis=0) * scale).astype(jnp.bfloat16)
    spread_piece = jnp.broadcast_to(piece[None], (peers,) + piece.shape)
    summed = lax.all_to_all(spread_piece, ("dom", "dev"), split_axis=0, concat_axis=0, tiled=True)
    summed = summed.reshape(partial.shape).astype(jnp.float32)
    grad_ws = summed[: w_self.shape[0]]
    grad_wn = summed[w_self.shape[0] :]
    hub_spread = jnp.broadcast_to(hub_pick[None], (group,) + hub_pick.shape)
    grad = lax.dot_general(dpre, w_self, contract_cols, preferred_element_type=jnp.float32) + own
    grad = grad + lax.dot_general(
        send_pick, returned.reshape(peers * slots, width), contract_rows, preferred_element_type=jnp.float32
    )
    grad = grad + lax.dot_general(
        hub_spread.reshape(group * hubs_dev, rows),
        hub_back.reshape(group * hubs_dev, width),
        contract_rows,
        preferred_element_type=jnp.float32,
    )
    return (out, grad.astype(jnp.bfloat16), grad_ws, grad_wn)


def solution(mesh):
    return jax.shard_map(
        body,
        mesh=mesh,
        in_specs=(
            P(("dom", "dev"), None),
            P(),
            P(),
            P(("dom", "dev"), None),
            P(("dom", "dev")),
            P(("dom", "dev"), None, None),
            P(("dom", "dev"), None),
            P(("dom", "dev")),
            P(("dom", "dev")),
            P(("dom", "dev")),
            P(("dom", "dev"), None, None),
        ),
        out_specs=(P(("dom", "dev"), None), P(("dom", "dev"), None), P(), P()),
        check_vma=False,
    )
```

```python
import functools

import jax
import jax.numpy as jnp
from jax import lax
from jax.experimental import pallas as pl
from jax.experimental.pallas import tpu as pltpu
from jax.sharding import PartitionSpec as P


def _tile_block(tiles):
    for size in (80, 64, 40, 32, 16, 8, 4, 2, 1):
        if tiles % size == 0:
            return size
    return 1


def _val_map(tb):
    def index_map(i, src, dst, cnt):
        last = jnp.maximum(cnt[0] - 1, 0) // tb
        return (jnp.minimum(i, last), 0, 0)
    return index_map

def _agg_kernel(src_ref, dst_ref, cnt_ref, val_ref, feats_ref, inc_ref, hub_ref, out_ref, acc_ref, source_ref, *, tb, edge, batch):
    i = pl.program_id(0)
    last_src = source_ref.shape[0] // edge - 1
    last_dst = acc_ref.shape[0] // edge - 1
    @pl.when(i == 0)
    def _():
        acc_ref[...] = jnp.zeros_like(acc_ref)
        own = feats_ref.shape[0]
        mid = own + inc_ref.shape[0]
        source_ref[:own, :] = feats_ref[...]
        source_ref[own:mid, :] = inc_ref[...]
        source_ref[mid:, :] = hub_ref[...]
    count = cnt_ref[0]
    def one(t, k):
        s = jnp.clip(src_ref[t], 0, last_src)
        x = source_ref[pl.ds(pl.multiple_of(s * edge, edge), edge), :]
        return jnp.dot(val_ref[k], x, preferred_element_type=jnp.float32)
    def add(t, term):
        d = jnp.clip(dst_ref[t], 0, last_dst)
        rows = pl.ds(pl.multiple_of(d * edge, edge), edge)
        acc_ref[rows, :] += term
    full = (i + 1) * tb <= count
    @pl.when(full)
    def _():
        for k0 in range(0, tb, batch):
            terms = [one(i * tb + k, k) for k in range(k0, k0 + batch)]
            for k, term in zip(range(k0, k0 + batch), terms):
                add(i * tb + k, term)
    @pl.when(jnp.logical_and(jnp.logical_not(full), i * tb < count))
    def _():
        def body(k, carry):
            t = i * tb + k
            @pl.when(t < count)
            def _():
                add(t, one(t, k))
            return carry
        lax.fori_loop(0, tb, body, 0)
    @pl.when(i == pl.num_programs(0) - 1)
    def _():
        width = acc_ref.shape[1]
        out_ref[:, :width] = source_ref[: acc_ref.shape[0], :]
        out_ref[:, width:] = acc_ref[...].astype(out_ref.dtype)

def tile_aggregate(tile_src, tile_dst, tile_count, tile_val, feats, incoming, hub_table, tb=16, batch=1):
    tiles, edge, _ = tile_val.shape
    rows, width = feats.shape
    src_rows = rows + incoming.shape[0] + hub_table.shape[0]
    kernel = functools.partial(_agg_kernel, tb=tb, edge=edge, batch=batch)
    whole = lambda i, s, d, c: (0, 0)
    return pl.pallas_call(
        kernel,
        out_shape=jax.ShapeDtypeStruct((rows, 2 * width), jnp.bfloat16),
        grid_spec=pltpu.PrefetchScalarGridSpec(
            num_scalar_prefetch=3, grid=(tiles // tb,),
            in_specs=[pl.BlockSpec((tb, edge, edge), _val_map(tb)),
                      pl.BlockSpec(feats.shape, whole),
                      pl.BlockSpec(incoming.shape, whole),
                      pl.BlockSpec(hub_table.shape, whole)],
            out_specs=pl.BlockSpec((rows, 2 * width), whole),
            scratch_shapes=[pltpu.VMEM((rows, width), jnp.float32),
                            pltpu.VMEM((src_rows, width), feats.dtype)]),
        compiler_params=pltpu.CompilerParams(dimension_semantics=("arbitrary",)),
    )(tile_src, tile_dst, tile_count, tile_val, feats, incoming, hub_table)


def _back_kernel(src_ref, dst_ref, cnt_ref, val_ref, dagg_ref, own_ref, ret_ref, hub_ref, acc_ref, *, tb, edge, batch):
    i = pl.program_id(0)
    last_src = acc_ref.shape[0] // edge - 1
    last_dst = dagg_ref.shape[0] // edge - 1
    rows = own_ref.shape[0]

    @pl.when(i == 0)
    def _():
        acc_ref[...] = jnp.zeros_like(acc_ref)

    count = cnt_ref[0]

    def one(t, k):
        d = jnp.clip(dst_ref[t], 0, last_dst)
        y = dagg_ref[pl.ds(pl.multiple_of(d * edge, edge), edge), :]
        return lax.dot_general(val_ref[k], y, (((0,), (0,)), ((), ())), preferred_element_type=jnp.float32)

    def add(t, term):
        s = jnp.clip(src_ref[t], 0, last_src)
        block = pl.ds(pl.multiple_of(s * edge, edge), edge)
        acc_ref[block, :] += term

    full = (i + 1) * tb <= count

    @pl.when(full)
    def _():
        for k0 in range(0, tb, batch):
            terms = [one(i * tb + k, k) for k in range(k0, k0 + batch)]
            for k, term in zip(range(k0, k0 + batch), terms):
                add(i * tb + k, term)

    @pl.when(jnp.logical_and(jnp.logical_not(full), i * tb < count))
    def _():
        def body(k, carry):
            t = i * tb + k

            @pl.when(t < count)
            def _():
                add(t, one(t, k))

            return carry

        lax.fori_loop(0, tb, body, 0)

    @pl.when(i == pl.num_programs(0) - 1)
    def _():
        split = rows + ret_ref.shape[0]
        own_ref[...] = acc_ref[:rows, :]
        ret_ref[...] = acc_ref[rows:split, :].astype(ret_ref.dtype)
        hub_ref[...] = acc_ref[split:, :].astype(hub_ref.dtype)


def tile_backward(tile_src, tile_dst, tile_count, tile_val, dagg, src_rows, ret_rows, tb=16, batch=1):
    tiles, edge, _ = tile_val.shape
    rows, width = dagg.shape
    kernel = functools.partial(_back_kernel, tb=tb, edge=edge, batch=batch)
    return pl.pallas_call(
        kernel,
        out_shape=(
            jax.ShapeDtypeStruct((rows, width), jnp.float32),
            jax.ShapeDtypeStruct((ret_rows, width), jnp.bfloat16),
            jax.ShapeDtypeStruct((src_rows - rows - ret_rows, width), jnp.bfloat16),
        ),
        grid_spec=pltpu.PrefetchScalarGridSpec(
            num_scalar_prefetch=3, grid=(tiles // tb,),
            in_specs=[pl.BlockSpec((tb, edge, edge), _val_map(tb)),
                      pl.BlockSpec(dagg.shape, lambda i, s, d, c: (0, 0))],
            out_specs=[pl.BlockSpec((rows, width), lambda i, s, d, c: (0, 0)),
                       pl.BlockSpec((ret_rows, width), lambda i, s, d, c: (0, 0)),
                       pl.BlockSpec((src_rows - rows - ret_rows, width), lambda i, s, d, c: (0, 0))],
            scratch_shapes=[pltpu.VMEM((src_rows, width), jnp.float32)]),
        compiler_params=pltpu.CompilerParams(dimension_semantics=("arbitrary",)),
    )(tile_src, tile_dst, tile_count, tile_val, dagg)


def one_hot_rows(index, count):
    columns = lax.broadcasted_iota(jnp.int32, (index.shape[0], count), 1)
    return (columns == index[:, None]).astype(jnp.bfloat16)


def body(
    feats,
    w_self,
    w_neigh,
    cotangent,
    hub_rows,
    send_rows,
    send_count,
    tile_dst,
    tile_src,
    tile_count,
    tile_val,
):
    edge = tile_val.shape[1]
    rows, width = feats.shape
    peers = send_rows.shape[1]
    slots = send_rows.shape[2]
    group = lax.axis_size("dev")
    hubs_dev = hub_rows.shape[0]

    hub_pick = one_hot_rows(hub_rows, rows)
    own_hubs = jnp.dot(hub_pick, feats, preferred_element_type=jnp.float32).astype(jnp.bfloat16)
    hub_out = jnp.broadcast_to(own_hubs[None], (group, hubs_dev, width))
    hub_table = lax.all_to_all(hub_out, "dev", split_axis=0, concat_axis=0, tiled=True)
    hub_table = hub_table.reshape(group * hubs_dev, width)

    live = lax.broadcasted_iota(jnp.int32, (peers, slots), 1) < send_count[0][:, None]
    send_pick = one_hot_rows(send_rows[0].reshape(-1), rows)
    send_pick = jnp.where(live.reshape(-1, 1), send_pick, jnp.zeros((), jnp.bfloat16))
    outgoing = jnp.dot(send_pick, feats, preferred_element_type=jnp.float32).astype(jnp.bfloat16)
    outgoing = outgoing.reshape(peers, slots, width)
    incoming = lax.all_to_all(outgoing, ("dom", "dev"), split_axis=0, concat_axis=0, tiled=True)
    incoming = incoming.reshape(peers * slots, width)
    src_rows = rows + incoming.shape[0] + hub_table.shape[0]

    tb = _tile_block(tile_val.shape[0])
    feats_agg = tile_aggregate(tile_src, tile_dst, tile_count, tile_val, feats, incoming, hub_table, tb=tb)

    w_both = jnp.concatenate([w_self, w_neigh], axis=0)
    pre = jnp.dot(feats_agg, w_both, preferred_element_type=jnp.float32)
    sig = jax.nn.sigmoid(pre)
    out = (pre * sig).astype(jnp.bfloat16)
    dpre = (cotangent.astype(jnp.float32) * sig * (1.0 + pre * (1.0 - sig))).astype(jnp.bfloat16)

    contract_rows = (((0,), (0,)), ((), ()))
    partial = lax.dot_general(feats_agg, dpre, contract_rows, preferred_element_type=jnp.float32)

    contract_cols = (((1,), (1,)), ((), ()))
    dagg = lax.dot_general(dpre, w_neigh, contract_cols, preferred_element_type=jnp.float32).astype(
        jnp.bfloat16
    )
    own, returning, hub_part = tile_backward(
        tile_src, tile_dst, tile_count, tile_val, dagg, src_rows, peers * slots, tb=tb
    )
    returning = returning.reshape(peers, slots, width)
    returned = lax.all_to_all(
        returning, ("dom", "dev"), split_axis=0, concat_axis=0, tiled=True
    )
    hub_back = lax.all_to_all(
        hub_part.reshape(group, hubs_dev, width),
        "dev",
        split_axis=0,
        concat_axis=0,
        tiled=True,
    )
    partial, returned, hub_back = lax.optimization_barrier((partial, returned, hub_back))
    parts = partial.reshape(peers, -1, width)
    gathered = lax.all_to_all(parts, ("dom", "dev"), split_axis=0, concat_axis=0, tiled=True)
    scale = 1.0 / jnp.sqrt(jnp.float32(rows * peers))
    piece = (jnp.sum(gathered, axis=0) * scale).astype(jnp.bfloat16)
    spread_piece = jnp.broadcast_to(piece[None], (peers,) + piece.shape)
    summed = lax.all_to_all(spread_piece, ("dom", "dev"), split_axis=0, concat_axis=0, tiled=True)
    summed = summed.reshape(partial.shape).astype(jnp.float32)
    grad_ws = summed[: w_self.shape[0]]
    grad_wn = summed[w_self.shape[0] :]
    hub_spread = jnp.broadcast_to(hub_pick[None], (group,) + hub_pick.shape)
    grad = lax.dot_general(dpre, w_self, contract_cols, preferred_element_type=jnp.float32) + own
    grad = grad + lax.dot_general(
        send_pick, returned.reshape(peers * slots, width), contract_rows, preferred_element_type=jnp.float32
    )
    grad = grad + lax.dot_general(
        hub_spread.reshape(group * hubs_dev, rows),
        hub_back.reshape(group * hubs_dev, width),
        contract_rows,
        preferred_element_type=jnp.float32,
    )
    return (out, grad.astype(jnp.bfloat16), grad_ws, grad_wn)


def solution(mesh):
    return jax.shard_map(
        body,
        mesh=mesh,
        in_specs=(
            P(("dom", "dev"), None),
            P(),
            P(),
            P(("dom", "dev"), None),
            P(("dom", "dev")),
            P(("dom", "dev"), None, None),
            P(("dom", "dev"), None),
            P(("dom", "dev")),
            P(("dom", "dev")),
            P(("dom", "dev")),
            P(("dom", "dev"), None, None),
        ),
        out_specs=(P(("dom", "dev"), None), P(("dom", "dev"), None), P(), P()),
        check_vma=False,
    )
```

```python
import functools

import jax
import jax.numpy as jnp
from jax import lax
from jax.experimental import pallas as pl
from jax.experimental.pallas import tpu as pltpu
from jax.sharding import PartitionSpec as P


def _tile_block(tiles):
    for size in (80, 64, 40, 32, 16, 8, 4, 2, 1):
        if tiles % size == 0:
            return size
    return 1


def _val_map(tb):
    def index_map(i, src, dst, cnt):
        last = jnp.maximum(cnt[0] - 1, 0) // tb
        return (jnp.minimum(i, last), 0, 0)
    return index_map

def _agg_kernel(src_ref, dst_ref, cnt_ref, val_ref, feats_ref, inc_ref, hub_ref, out_ref, acc_ref, source_ref, *, tb, edge, batch):
    i = pl.program_id(0)
    last_src = source_ref.shape[0] // edge - 1
    last_dst = acc_ref.shape[0] // edge - 1
    @pl.when(i == 0)
    def _():
        acc_ref[...] = jnp.zeros_like(acc_ref)
        own = feats_ref.shape[0]
        mid = own + inc_ref.shape[0]
        source_ref[:own, :] = feats_ref[...]
        source_ref[own:mid, :] = inc_ref[...]
        source_ref[mid:, :] = hub_ref[...]
    count = cnt_ref[0]
    def one(t, k):
        s = jnp.clip(src_ref[t], 0, last_src)
        x = source_ref[pl.ds(pl.multiple_of(s * edge, edge), edge), :]
        return jnp.dot(val_ref[k], x, preferred_element_type=jnp.float32)
    def add(t, term):
        d = jnp.clip(dst_ref[t], 0, last_dst)
        rows = pl.ds(pl.multiple_of(d * edge, edge), edge)
        acc_ref[rows, :] += term
    full = (i + 1) * tb <= count
    @pl.when(full)
    def _():
        for k0 in range(0, tb, batch):
            terms = [one(i * tb + k, k) for k in range(k0, k0 + batch)]
            for k, term in zip(range(k0, k0 + batch), terms):
                add(i * tb + k, term)
    @pl.when(jnp.logical_and(jnp.logical_not(full), i * tb < count))
    def _():
        def body(k, carry):
            t = i * tb + k
            @pl.when(t < count)
            def _():
                add(t, one(t, k))
            return carry
        lax.fori_loop(0, tb, body, 0)
    @pl.when(i == pl.num_programs(0) - 1)
    def _():
        width = acc_ref.shape[1]
        out_ref[:, :width] = source_ref[: acc_ref.shape[0], :]
        out_ref[:, width:] = acc_ref[...].astype(out_ref.dtype)

def tile_aggregate(tile_src, tile_dst, tile_count, tile_val, feats, incoming, hub_table, tb=16, batch=1):
    tiles, edge, _ = tile_val.shape
    rows, width = feats.shape
    src_rows = rows + incoming.shape[0] + hub_table.shape[0]
    kernel = functools.partial(_agg_kernel, tb=tb, edge=edge, batch=batch)
    whole = lambda i, s, d, c: (0, 0)
    return pl.pallas_call(
        kernel,
        out_shape=jax.ShapeDtypeStruct((rows, 2 * width), jnp.bfloat16),
        grid_spec=pltpu.PrefetchScalarGridSpec(
            num_scalar_prefetch=3, grid=(tiles // tb,),
            in_specs=[pl.BlockSpec((tb, edge, edge), _val_map(tb)),
                      pl.BlockSpec(feats.shape, whole),
                      pl.BlockSpec(incoming.shape, whole),
                      pl.BlockSpec(hub_table.shape, whole)],
            out_specs=pl.BlockSpec((rows, 2 * width), whole),
            scratch_shapes=[pltpu.VMEM((rows, width), jnp.float32),
                            pltpu.VMEM((src_rows, width), feats.dtype)]),
        compiler_params=pltpu.CompilerParams(dimension_semantics=("arbitrary",)),
    )(tile_src, tile_dst, tile_count, tile_val, feats, incoming, hub_table)


def _back_kernel(src_ref, dst_ref, cnt_ref, val_ref, dagg_ref, own_ref, ret_ref, hub_ref, acc_ref, *, tb, edge, batch):
    i = pl.program_id(0)
    last_src = acc_ref.shape[0] // edge - 1
    last_dst = dagg_ref.shape[0] // edge - 1
    rows = own_ref.shape[0]

    @pl.when(i == 0)
    def _():
        acc_ref[...] = jnp.zeros_like(acc_ref)

    count = cnt_ref[0]

    def one(t, k):
        d = jnp.clip(dst_ref[t], 0, last_dst)
        y = dagg_ref[pl.ds(pl.multiple_of(d * edge, edge), edge), :]
        return lax.dot_general(val_ref[k], y, (((0,), (0,)), ((), ())), preferred_element_type=jnp.float32)

    def add(t, term):
        s = jnp.clip(src_ref[t], 0, last_src)
        block = pl.ds(pl.multiple_of(s * edge, edge), edge)
        acc_ref[block, :] += term

    full = (i + 1) * tb <= count

    @pl.when(full)
    def _():
        for k0 in range(0, tb, batch):
            terms = [one(i * tb + k, k) for k in range(k0, k0 + batch)]
            for k, term in zip(range(k0, k0 + batch), terms):
                add(i * tb + k, term)

    @pl.when(jnp.logical_and(jnp.logical_not(full), i * tb < count))
    def _():
        def body(k, carry):
            t = i * tb + k

            @pl.when(t < count)
            def _():
                add(t, one(t, k))

            return carry

        lax.fori_loop(0, tb, body, 0)

    @pl.when(i == pl.num_programs(0) - 1)
    def _():
        split = rows + ret_ref.shape[0]
        own_ref[...] = acc_ref[:rows, :]
        ret_ref[...] = acc_ref[rows:split, :].astype(ret_ref.dtype)
        hub_ref[...] = acc_ref[split:, :].astype(hub_ref.dtype)


def tile_backward(tile_src, tile_dst, tile_count, tile_val, dagg, src_rows, ret_rows, tb=16, batch=1):
    tiles, edge, _ = tile_val.shape
    rows, width = dagg.shape
    kernel = functools.partial(_back_kernel, tb=tb, edge=edge, batch=batch)
    return pl.pallas_call(
        kernel,
        out_shape=(
            jax.ShapeDtypeStruct((rows, width), jnp.float32),
            jax.ShapeDtypeStruct((ret_rows, width), jnp.bfloat16),
            jax.ShapeDtypeStruct((src_rows - rows - ret_rows, width), jnp.bfloat16),
        ),
        grid_spec=pltpu.PrefetchScalarGridSpec(
            num_scalar_prefetch=3, grid=(tiles // tb,),
            in_specs=[pl.BlockSpec((tb, edge, edge), _val_map(tb)),
                      pl.BlockSpec(dagg.shape, lambda i, s, d, c: (0, 0))],
            out_specs=[pl.BlockSpec((rows, width), lambda i, s, d, c: (0, 0)),
                       pl.BlockSpec((ret_rows, width), lambda i, s, d, c: (0, 0)),
                       pl.BlockSpec((src_rows - rows - ret_rows, width), lambda i, s, d, c: (0, 0))],
            scratch_shapes=[pltpu.VMEM((src_rows, width), jnp.float32)]),
        compiler_params=pltpu.CompilerParams(dimension_semantics=("arbitrary",)),
    )(tile_src, tile_dst, tile_count, tile_val, dagg)


def one_hot_rows(index, count):
    columns = lax.broadcasted_iota(jnp.int32, (index.shape[0], count), 1)
    return (columns == index[:, None]).astype(jnp.bfloat16)


def body(
    feats,
    w_self,
    w_neigh,
    cotangent,
    hub_rows,
    send_rows,
    send_count,
    tile_dst,
    tile_src,
    tile_count,
    tile_val,
):
    edge = tile_val.shape[1]
    rows, width = feats.shape
    peers = send_rows.shape[1]
    slots = send_rows.shape[2]
    group = lax.axis_size("dev")
    hubs_dev = hub_rows.shape[0]

    hub_pick = one_hot_rows(hub_rows, rows)
    own_hubs = jnp.dot(hub_pick, feats, preferred_element_type=jnp.float32).astype(jnp.bfloat16)
    hub_out = jnp.broadcast_to(own_hubs[None], (group, hubs_dev, width))
    hub_table = lax.all_to_all(hub_out, "dev", split_axis=0, concat_axis=0, tiled=True)
    hub_table = hub_table.reshape(group * hubs_dev, width)

    live = lax.broadcasted_iota(jnp.int32, (peers, slots), 1) < send_count[0][:, None]
    send_index = jnp.where(live, send_rows[0], jnp.int32(-1))
    send_pick = one_hot_rows(send_index.reshape(-1), rows)
    outgoing = jnp.dot(send_pick, feats, preferred_element_type=jnp.float32).astype(jnp.bfloat16)
    outgoing = outgoing.reshape(peers, slots, width)
    incoming = lax.all_to_all(outgoing, ("dom", "dev"), split_axis=0, concat_axis=0, tiled=True)
    incoming = incoming.reshape(peers * slots, width)
    src_rows = rows + incoming.shape[0] + hub_table.shape[0]

    tb = _tile_block(tile_val.shape[0])
    feats_agg = tile_aggregate(tile_src, tile_dst, tile_count, tile_val, feats, incoming, hub_table, tb=tb)

    w_both = jnp.concatenate([w_self, w_neigh], axis=0)
    pre = jnp.dot(feats_agg, w_both, preferred_element_type=jnp.float32)
    sig = jax.nn.sigmoid(pre)
    out = (pre * sig).astype(jnp.bfloat16)
    dpre = (cotangent.astype(jnp.float32) * sig * (1.0 + pre * (1.0 - sig))).astype(jnp.bfloat16)

    contract_rows = (((0,), (0,)), ((), ()))
    partial = lax.dot_general(feats_agg, dpre, contract_rows, preferred_element_type=jnp.float32)

    contract_cols = (((1,), (1,)), ((), ()))
    dagg = lax.dot_general(dpre, w_neigh, contract_cols, preferred_element_type=jnp.float32).astype(
        jnp.bfloat16
    )
    own, returning, hub_part = tile_backward(
        tile_src, tile_dst, tile_count, tile_val, dagg, src_rows, peers * slots, tb=tb
    )
    returning = returning.reshape(peers, slots, width)
    returned = lax.all_to_all(
        returning, ("dom", "dev"), split_axis=0, concat_axis=0, tiled=True
    )
    hub_back = lax.all_to_all(
        hub_part.reshape(group, hubs_dev, width),
        "dev",
        split_axis=0,
        concat_axis=0,
        tiled=True,
    )
    partial, returned, hub_back = lax.optimization_barrier((partial, returned, hub_back))
    parts = partial.reshape(peers, -1, width)
    gathered = lax.all_to_all(parts, ("dom", "dev"), split_axis=0, concat_axis=0, tiled=True)
    scale = 1.0 / jnp.sqrt(jnp.float32(rows * peers))
    piece = (jnp.sum(gathered, axis=0) * scale).astype(jnp.bfloat16)
    spread_piece = jnp.broadcast_to(piece[None], (peers,) + piece.shape)
    summed = lax.all_to_all(spread_piece, ("dom", "dev"), split_axis=0, concat_axis=0, tiled=True)
    summed = summed.reshape(partial.shape).astype(jnp.float32)
    grad_ws = summed[: w_self.shape[0]]
    grad_wn = summed[w_self.shape[0] :]
    hub_spread = jnp.broadcast_to(hub_pick[None], (group,) + hub_pick.shape)
    grad = lax.dot_general(dpre, w_self, contract_cols, preferred_element_type=jnp.float32) + own
    grad = grad + lax.dot_general(
        send_pick, returned.reshape(peers * slots, width), contract_rows, preferred_element_type=jnp.float32
    )
    grad = grad + lax.dot_general(
        hub_spread.reshape(group * hubs_dev, rows),
        hub_back.reshape(group * hubs_dev, width),
        contract_rows,
        preferred_element_type=jnp.float32,
    )
    return (out, grad.astype(jnp.bfloat16), grad_ws, grad_wn)


def solution(mesh):
    return jax.shard_map(
        body,
        mesh=mesh,
        in_specs=(
            P(("dom", "dev"), None),
            P(),
            P(),
            P(("dom", "dev"), None),
            P(("dom", "dev")),
            P(("dom", "dev"), None, None),
            P(("dom", "dev"), None),
            P(("dom", "dev")),
            P(("dom", "dev")),
            P(("dom", "dev")),
            P(("dom", "dev"), None, None),
        ),
        out_specs=(P(("dom", "dev"), None), P(("dom", "dev"), None), P(), P()),
        check_vma=False,
    )
```
